256 devices in a mesh: gy: 8 (over y, x_hi), gx: 4 (over x_lo, core), wa: 8 (over z).
Axes of the slice: x: 4 (x_hi: 2, x_lo: 2; x = x_hi * 2 + x_lo), y: 4, z: 8, core: 2. Of those that a mesh axis runs over, the one named last changes fastest.
Arguments:
- tokens: bfloat16 [8, 64, 128, 3072], P('wa', 'gy', 'gx'), may hold values from -6 to 6
- mod_shift: float32 [8, 3072], P('wa'), may hold values from -3 to 3
- mod_scale: float32 [8, 3072], P('wa'), may hold values from -0.9 to 3.9
- qkv_weight: bfloat16 [3072, 4608], P(None, ('gx', 'wa')), may hold values from -0.14433757 to 0.14433757
- block_codes: int32 [8, 16, 9], P('gy', 'gx'), may hold values from 0 to 8, as said below
- block_counts: int32 [8, 16], P('gy', 'gx'), may hold values from 1 to 9, as said below
- valid_tokens: int32 [8, 16], replicated, may hold values from 1 to 64
Outputs:
- attended: bfloat16 [8, 64, 128, 1536], P('wa', 'gy', 'gx')
The draws below stay inside these ranges and needn't reach their ends.
Inputs may be any that keep to these rules, and one draw needn't show every extreme that they name: `block_codes`: the 9 codes of a block's list are distinct, the first is 4 (the block itself), and the first block_counts entries name blocks inside the grid. `block_counts`: A count never exceeds the number of blocks of the 3 x 3 neighbourhood that lie inside the grid.
All inputs are finite; a program needn't handle non-finite values.
Results may differ from the reference program's by a relative error of at most 0.007.
Values may be sent and summed in bfloat16 or wider, within the bound.
No kernel may reach another device: no remote copies, remote signals or barrier semaphores. Data moves between devices by JAX's collectives and lax.ppermute only.
A program may use at most 128 MiB of HBM per device.

```python
import math
import jax
import jax.numpy as jnp
from jax import lax

D = 3072
HEADS = 12
HD = 128
BLK = 8
NBR = 9
SAMPLES = 8
GH = 64
GW = 128
BROWS = 8
BCOLS = 16


def plan_blocks(key):
    folded = jax.random.fold_in(key, 11)
    key_rank, key_count = jax.random.split(folded)
    offsets = jnp.arange(NBR, dtype=jnp.int32)
    row_step = offsets // 3 - 1
    col_step = offsets % 3 - 1
    row_ids = jnp.arange(BROWS, dtype=jnp.int32)[:, None, None]
    col_ids = jnp.arange(BCOLS, dtype=jnp.int32)[None, :, None]
    inside = (row_ids + row_step >= 0) & (row_ids + row_step < BROWS) & (col_ids + col_step >= 0) & (col_ids + col_step < BCOLS)
    ranking = jax.random.randint(key_rank, (BROWS, BCOLS, NBR), 0, 1 << 20)
    ranking = jnp.where(offsets == 4, -1, ranking)
    order_key = ranking * 16 + offsets + jnp.where(inside, 0, 1 << 26)
    codes = jnp.argsort(order_key, axis=-1).astype(jnp.int32)
    reachable = jnp.sum(inside.astype(jnp.int32), axis=-1).astype(jnp.int32)
    picked = jax.random.randint(key_count, (BROWS, BCOLS), 1, NBR + 1).astype(jnp.int32)
    counts = jnp.minimum(picked, reachable)
    counts = counts.at[1, 1].set(reachable[1, 1])
    return (codes, counts)


def draw_block_codes(key, part):
    return plan_blocks(key)[0]


def draw_block_counts(key, part):
    return plan_blocks(key)[1]


def draw_valid_tokens(key, part):
    folded = jax.random.fold_in(key, 23)
    drawn = jax.random.randint(folded, (BROWS, BCOLS), 1, BLK * BLK + 1).astype(jnp.int32)
    row_ids = jnp.arange(BROWS, dtype=jnp.int32)[:, None]
    col_ids = jnp.arange(BCOLS, dtype=jnp.int32)[None, :]
    border = (row_ids == BROWS - 1) | (col_ids == BCOLS - 1)
    result = jnp.where(border, drawn, BLK * BLK).astype(jnp.int32)
    return result.at[BROWS - 1, BCOLS - 1].set(1)


def draw_mod_scale(key, part):
    folded = jax.random.fold_in(key, 31)
    noise = jax.random.normal(folded, (SAMPLES, D), jnp.float32)
    value = 0.3 * noise
    return jnp.clip(value, -0.9, 3.9).astype(jnp.float32)


def draw_qkv_weight(key, part):
    folded = jax.random.fold_in(key, 41)
    normal_part = jax.random.truncated_normal(folded, -6.0, 6.0, (D, 3 * HEADS * HD), jnp.float32) * (1.0 / math.sqrt(D))
    return normal_part.astype(jnp.bfloat16)


def shard_levels(rng, extent, pieces, least, high):
    factor_of, own = 1.0, jax.random.fold_in(rng, 6)
    for axis_at, shards_of in pieces:
        steps = jnp.exp(jax.random.uniform(jax.random.fold_in(own, axis_at), (shards_of,), jnp.float32, least / len(pieces), high / len(pieces)))
        factor_of = factor_of * jnp.repeat(steps, extent[axis_at] // shards_of).reshape([-1 if axis == axis_at else 1 for axis in range(len(extent))])
    return factor_of


def normal_values(rng, extent, scale, reach, shards=(), held_as=jnp.bfloat16):
    factor_of = shard_levels(rng, extent, shards, -0.22, 0.18) if shards else 1.0
    values = jax.random.normal(rng, extent, jnp.float32) * scale * factor_of
    return jnp.minimum(jnp.maximum(values, -reach), reach).astype(held_as)


def setup_inputs(seed: int = 0) -> dict:
    arg_keys = jax.random.split(jax.random.key(seed), 8)
    tokens = normal_values(arg_keys[0], (SAMPLES, GH, GW, D), 1.0, 6.0, ((0, 8), (1, 8), (2, 4)))
    mod_shift = normal_values(arg_keys[1], (SAMPLES, D), 0.5, 3.0, ((0, 8),), jnp.float32)
    mod_scale = draw_mod_scale(jax.random.fold_in(arg_keys[7], 71), 0)
    qkv_weight = draw_qkv_weight(jax.random.fold_in(arg_keys[7], 71), 0)
    block_codes = draw_block_codes(jax.random.fold_in(arg_keys[7], 71), 0)
    block_counts = draw_block_counts(jax.random.fold_in(arg_keys[7], 71), 0)
    valid_tokens = draw_valid_tokens(jax.random.fold_in(arg_keys[7], 71), 0)
    return {"tokens": tokens, "mod_shift": mod_shift, "mod_scale": mod_scale, "qkv_weight": qkv_weight, "block_codes": block_codes, "block_counts": block_counts, "valid_tokens": valid_tokens}


def normalize(rows, shift_row, scale_row):
    widened = rows.astype(jnp.float32)
    average = lax.optimization_barrier(jnp.mean(widened, axis=-1, keepdims=True))
    centred = widened - average
    spread = lax.optimization_barrier(jnp.mean(centred * centred, axis=-1, keepdims=True))
    return (centred * lax.rsqrt(spread + 1e-06) * (1.0 + scale_row) + shift_row).astype(jnp.bfloat16)

def to_blocks(field):
    height, breadth, channels = field.shape
    shaped = field.reshape(height // BLK, BLK, breadth // BLK, BLK, channels)
    return shaped.transpose(0, 2, 1, 3, 4).reshape(height // BLK, breadth // BLK, BLK * BLK, channels)

def from_blocks(blocks):
    block_rows, block_cols, cells, channels = blocks.shape
    shaped = blocks.reshape(block_rows, block_cols, BLK, BLK, channels)
    return shaped.transpose(0, 2, 1, 3, 4).reshape(block_rows * BLK, block_cols * BLK, channels)

def make_mask(counts, live_count):
    slot_ids = jnp.arange(NBR, dtype=jnp.int32)
    token_ids = jnp.arange(BLK * BLK, dtype=jnp.int32)
    used = slot_ids[:, None] < counts[..., None, None]
    return used & (token_ids < live_count[..., None])

def attend(queries, key_blocks, key_mask):
    number = queries.shape[0]
    query_heads = queries.reshape(number, BLK * BLK, HEADS, HD).astype(jnp.float32)
    key_value = key_blocks.reshape(number, NBR * BLK * BLK, 2, HEADS, HD).astype(jnp.float32)
    scores = jnp.einsum('nqhd,nkhd->nhqk', query_heads, key_value[:, :, 0]) * (1.0 / math.sqrt(HD))
    scores = jnp.where(key_mask[:, None, None, :], scores, -jnp.inf)
    highest = lax.optimization_barrier(jnp.max(scores, axis=-1, keepdims=True))
    exponent = jnp.exp(scores - highest)
    probs = (exponent / lax.optimization_barrier(jnp.sum(exponent, axis=-1, keepdims=True))).astype(jnp.bfloat16)
    blended = jnp.einsum('nhqk,nkhd->nqhd', probs.astype(jnp.float32), key_value[:, :, 1])
    return blended.astype(jnp.bfloat16).reshape(number, BLK * BLK, HEADS * HD)

def reference(tokens, mod_shift, mod_scale, qkv_weight, block_codes, block_counts, valid_tokens):
    width = HEADS * HD

    def one_sample(inputs):
        sample_tokens, shift_row, scale_row = inputs
        normed = normalize(sample_tokens, shift_row, scale_row).reshape(GH * GW, D)
        qkv = jnp.dot(normed, qkv_weight, preferred_element_type=jnp.float32).astype(jnp.bfloat16)
        qkv_grid = qkv.reshape(GH, GW, 3 * width)
        queries = to_blocks(qkv_grid[:, :, :width])
        key_blocks = jnp.pad(to_blocks(qkv_grid[:, :, width:]), ((1, 1), (1, 1), (0, 0), (0, 0)))
        col_ids = jnp.arange(BCOLS, dtype=jnp.int32)[:, None]

        def one_row(index_row):
            codes = block_codes[index_row]
            row_step = codes // 3 - 1
            col_step = codes % 3 - 1
            picked = key_blocks[index_row + 1 + row_step, col_ids + 1 + col_step]
            global_row = jnp.clip(index_row + row_step, 0, BROWS - 1)
            global_col = jnp.clip(col_ids + col_step, 0, BCOLS - 1)
            live_count = valid_tokens[global_row, global_col]
            key_mask = make_mask(block_counts[index_row], live_count)
            return attend(queries[index_row], picked, key_mask.reshape(BCOLS, NBR * BLK * BLK))
        result = lax.map(one_row, jnp.arange(BROWS, dtype=jnp.int32))
        return from_blocks(result)
    return lax.map(one_sample, (tokens, mod_shift, mod_scale))
```

```python
import math

import jax
import jax.numpy as jnp
from jax import lax
from jax.sharding import PartitionSpec as P

D = 3072
HEADS = 12
HD = 128
BLK = 8
NBR = 9


def extended_2(array, sides, width):
    for axis, dim in sides:
        size, length = (lax.axis_size(axis), array.shape[dim])
        up = [(i, (i + 1) % size) for i in range(size - 1)]
        down = [(j, i) for i, j in up]
        last = lax.slice_in_dim(array, length - width, length, axis=dim)
        first = lax.slice_in_dim(array, 0, width, axis=dim)
        before = lax.ppermute(last, axis, up)
        after = lax.ppermute(first, axis, down)
        array = jnp.concatenate([before, array, after], axis=dim)
    return array


def normalize(rows, shift_row, scale_row):
    widened = rows.astype(jnp.float32)
    average = jnp.mean(widened, axis=-1, keepdims=True)
    centred = widened - average
    spread = jnp.mean(centred * centred, axis=-1, keepdims=True)
    return (centred * lax.rsqrt(spread + 1e-06) * (1.0 + scale_row) + shift_row).astype(
        jnp.bfloat16
    )


def to_blocks(field):
    height, breadth, channels = field.shape
    shaped = field.reshape(height // BLK, BLK, breadth // BLK, BLK, channels)
    return shaped.transpose(0, 2, 1, 3, 4).reshape(
        height // BLK, breadth // BLK, BLK * BLK, channels
    )


def from_blocks(blocks):
    block_rows, block_cols, cells, channels = blocks.shape
    shaped = blocks.reshape(block_rows, block_cols, BLK, BLK, channels)
    return shaped.transpose(0, 2, 1, 3, 4).reshape(block_rows * BLK, block_cols * BLK, channels)


def make_mask(counts, live_count):
    slot_ids = jnp.arange(NBR, dtype=jnp.int32)
    token_ids = jnp.arange(BLK * BLK, dtype=jnp.int32)
    used = slot_ids[:, None] < counts[..., None, None]
    return used & (token_ids < live_count[..., None])


def attend(queries, key_blocks, key_mask):
    number = queries.shape[0]
    query_heads = queries.reshape(number, BLK * BLK, HEADS, HD)
    key_value = key_blocks.reshape(number, NBR * BLK * BLK, 2, HEADS, HD)
    scores = jnp.einsum(
        "nqhd,nkhd->nhqk", query_heads, key_value[:, :, 0], preferred_element_type=jnp.float32
    ) * (1.0 / math.sqrt(HD))
    scores = jnp.where(key_mask[:, None, None, :], scores, -jnp.inf)
    highest = jnp.max(scores, axis=-1, keepdims=True)
    exponent = jnp.exp(scores - highest)
    probs = (exponent / jnp.sum(exponent, axis=-1, keepdims=True)).astype(jnp.bfloat16)
    blended = jnp.einsum(
        "nhqk,nkhd->nqhd", probs, key_value[:, :, 1], preferred_element_type=jnp.float32
    )
    return blended.astype(jnp.bfloat16).reshape(number, BLK * BLK, HEADS * HD)


def body(tokens, mod_shift, mod_scale, qkv_weight, block_codes, block_counts, valid_tokens):
    tile_rows = tokens.shape[1]
    tile_cols = tokens.shape[2]
    width = HEADS * HD
    weight_block = lax.all_gather(qkv_weight, "wa", axis=1, tiled=True)
    flat_rows = normalize(tokens[0], mod_shift[0], mod_scale[0]).reshape(tile_rows * tile_cols, D)
    row_group = lax.all_gather(flat_rows, "gx", axis=0, tiled=True)
    partial = jnp.dot(row_group, weight_block, preferred_element_type=jnp.float32).astype(
        jnp.bfloat16
    )
    qkv = lax.all_to_all(partial, "gx", 0, 1, tiled=True)
    qkv_grid = qkv.reshape(tile_rows, tile_cols, 3 * width)
    extended = extended_2(qkv_grid[:, :, width:], (("gy", 0), ("gx", 1)), BLK)
    block_rows = tile_rows // BLK
    block_cols = tile_cols // BLK
    queries = to_blocks(qkv_grid[:, :, :width])
    key_blocks = to_blocks(extended)
    row_ids = jnp.arange(block_rows, dtype=jnp.int32)[:, None, None]
    col_ids = jnp.arange(block_cols, dtype=jnp.int32)[None, :, None]
    row_step = block_codes // 3 - 1
    col_step = block_codes % 3 - 1
    picked = key_blocks[row_ids + 1 + row_step, col_ids + 1 + col_step]
    global_row = jnp.clip(
        lax.axis_index("gy") * block_rows + row_ids + row_step, 0, valid_tokens.shape[0] - 1
    )
    global_col = jnp.clip(
        lax.axis_index("gx") * block_cols + col_ids + col_step, 0, valid_tokens.shape[1] - 1
    )
    live_count = valid_tokens[global_row, global_col]
    key_mask = make_mask(block_counts, live_count)
    number = block_rows * block_cols
    result = attend(
        queries.reshape(number, BLK * BLK, width),
        picked.reshape(number, NBR, BLK * BLK, 2 * width),
        key_mask.reshape(number, NBR * BLK * BLK),
    )
    return from_blocks(result.reshape(block_rows, block_cols, BLK * BLK, width))[None]


def solution(mesh):
    return jax.shard_map(
        body,
        mesh=mesh,
        in_specs=(
            P("wa", "gy", "gx", None),
            P("wa", None),
            P("wa", None),
            P(None, ("gx", "wa")),
            P("gy", "gx", None),
            P("gy", "gx"),
            P(),
        ),
        out_specs=P("wa", "gy", "gx", None),
        check_vma=False,
    )
```

```python
import functools
import math

import jax
import jax.numpy as jnp
from jax import lax
from jax.experimental import pallas as pl
from jax.experimental.pallas import tpu as pltpu
from jax.sharding import PartitionSpec as P

D = 3072
HEADS = 12
HD = 128
BLK = 8
NBR = 9
CELLS = BLK * BLK


def extended_2(array, sides, width):
    for axis, dim in sides:
        size, length = (lax.axis_size(axis), array.shape[dim])
        up = [(i, (i + 1) % size) for i in range(size - 1)]
        down = [(j, i) for i, j in up]
        last = lax.slice_in_dim(array, length - width, length, axis=dim)
        first = lax.slice_in_dim(array, 0, width, axis=dim)
        before = lax.ppermute(last, axis, up)
        after = lax.ppermute(first, axis, down)
        array = jnp.concatenate([before, array, after], axis=dim)
    return array


def normalize(rows, shift_row, scale_row):
    widened = rows.astype(jnp.float32)
    average = jnp.mean(widened, axis=-1, keepdims=True)
    centred = widened - average
    spread = jnp.mean(centred * centred, axis=-1, keepdims=True)
    return (centred * lax.rsqrt(spread + 1e-06) * (1.0 + scale_row) + shift_row).astype(
        jnp.bfloat16
    )


def to_blocks(field):
    height, breadth, channels = field.shape
    shaped = field.reshape(height // BLK, BLK, breadth // BLK, BLK, channels)
    return shaped.transpose(0, 2, 1, 3, 4).reshape(
        height // BLK, breadth // BLK, BLK * BLK, channels
    )


def from_blocks(blocks):
    block_rows, block_cols, cells, channels = blocks.shape
    shaped = blocks.reshape(block_rows, block_cols, BLK, BLK, channels)
    return shaped.transpose(0, 2, 1, 3, 4).reshape(block_rows * BLK, block_cols * BLK, channels)


def attend_kernel(block_cols, codes_ref, counts_ref, live_ref, q_ref, kv_hbm, o_ref, kv_buf, sems):
    j = pl.program_id(0)
    n_blocks = pl.num_programs(0)
    ext_cols = block_cols + 2

    def copies(block, slot):
        out = []
        for l in range(NBR):
            code = jnp.clip(codes_ref[block * NBR + l], 0, NBR - 1)
            src = (block // block_cols + code // 3) * ext_cols + block % block_cols + code % 3
            out.append(
                pltpu.make_async_copy(
                    kv_hbm.at[src], kv_buf.at[slot, pl.ds(l * CELLS, CELLS)], sems.at[slot, l]
                )
            )
        return out

    @pl.when(j == 0)
    def _():
        for c in copies(j, 0):
            c.start()

    slot = j % 2

    @pl.when(j + 1 < n_blocks)
    def _():
        for c in copies(j + 1, 1 - slot):
            c.start()

    for c in copies(j, slot):
        c.wait()

    count = counts_ref[j]
    key_ids = lax.broadcasted_iota(jnp.int32, (CELLS, NBR * CELLS), 1)
    key_slot = key_ids // CELLS
    key_token = key_ids % CELLS
    limit = jnp.zeros((CELLS, NBR * CELLS), jnp.int32)
    for l in range(NBR):
        thr = jnp.where(l < count, live_ref[j * NBR + l], 0)
        limit = jnp.where(key_slot == l, thr, limit)
    live = key_token < limit
    width = HEADS * HD
    for h in range(HEADS):
        q = q_ref[0, :, h * HD:(h + 1) * HD]
        k = kv_buf[slot, :, h * HD:(h + 1) * HD]
        v = kv_buf[slot, :, width + h * HD:width + (h + 1) * HD]
        s = lax.dot_general(
            q, k, (((1,), (1,)), ((), ())), preferred_element_type=jnp.float32
        ) * (1.0 / math.sqrt(HD))
        s = jnp.where(live, s, -jnp.inf)
        m = jnp.max(s, axis=-1, keepdims=True)
        e = jnp.exp(s - m)
        p = (e / jnp.sum(e, axis=-1, keepdims=True)).astype(jnp.bfloat16)
        o = jnp.dot(p, v, preferred_element_type=jnp.float32)
        o_ref[0, :, h * HD:(h + 1) * HD] = o.astype(o_ref.dtype)


def local_attention(q_blocks, kv_blocks, codes, counts, live_count, block_cols):
    n_blocks = q_blocks.shape[0]
    width = q_blocks.shape[-1]
    grid_spec = pltpu.PrefetchScalarGridSpec(
        num_scalar_prefetch=3,
        grid=(n_blocks,),
        in_specs=[
            pl.BlockSpec((1, CELLS, width), lambda j, *_: (j, 0, 0)),
            pl.BlockSpec(memory_space=pl.ANY),
        ],
        out_specs=pl.BlockSpec((1, CELLS, width), lambda j, *_: (j, 0, 0)),
        scratch_shapes=[
            pltpu.VMEM((2, NBR * CELLS, 2 * width), jnp.bfloat16),
            pltpu.SemaphoreType.DMA((2, NBR)),
        ],
    )
    return pl.pallas_call(
        functools.partial(attend_kernel, block_cols),
        grid_spec=grid_spec,
        out_shape=jax.ShapeDtypeStruct(q_blocks.shape, jnp.bfloat16),
        compiler_params=pltpu.CompilerParams(dimension_semantics=("arbitrary",)),
    )(codes.reshape(-1), counts.reshape(-1), live_count.reshape(-1), q_blocks, kv_blocks)


def body(tokens, mod_shift, mod_scale, qkv_weight, block_codes, block_counts, valid_tokens):
    tile_rows = tokens.shape[1]
    tile_cols = tokens.shape[2]
    width = HEADS * HD
    flat_rows = normalize(tokens[0], mod_shift[0], mod_scale[0]).reshape(tile_rows * tile_cols, D)
    qkv = jnp.dot(
        flat_rows,
        lax.all_gather(qkv_weight, ("gx", "wa"), axis=1, tiled=True),
        preferred_element_type=jnp.float32,
    ).astype(jnp.bfloat16)
    qkv_grid = qkv.reshape(tile_rows, tile_cols, 3 * width)
    extended = extended_2(qkv_grid[:, :, width:], (("gy", 0), ("gx", 1)), BLK)
    block_rows = tile_rows // BLK
    block_cols = tile_cols // BLK
    queries = to_blocks(qkv_grid[:, :, :width])
    key_blocks = to_blocks(extended)
    row_ids = jnp.arange(block_rows, dtype=jnp.int32)[:, None, None]
    col_ids = jnp.arange(block_cols, dtype=jnp.int32)[None, :, None]
    row_step = block_codes // 3 - 1
    col_step = block_codes % 3 - 1
    global_row = jnp.clip(
        lax.axis_index("gy") * block_rows + row_ids + row_step, 0, valid_tokens.shape[0] - 1
    )
    global_col = jnp.clip(
        lax.axis_index("gx") * block_cols + col_ids + col_step, 0, valid_tokens.shape[1] - 1
    )
    live_count = valid_tokens[global_row, global_col]
    number = block_rows * block_cols
    result = local_attention(
        queries.reshape(number, CELLS, width),
        key_blocks.reshape(-1, CELLS, 2 * width),
        block_codes.reshape(number, NBR),
        block_counts.reshape(number),
        live_count.reshape(number, NBR),
        block_cols,
    )
    return from_blocks(result.reshape(block_rows, block_cols, CELLS, width))[None]


def solution(mesh):
    return jax.shard_map(
        body,
        mesh=mesh,
        in_specs=(
            P("wa", "gy", "gx", None),
            P("wa", None),
            P("wa", None),
            P(None, ("gx", "wa")),
            P("gy", "gx", None),
            P("gy", "gx"),
            P(),
        ),
        out_specs=P("wa", "gy", "gx", None),
        check_vma=False,
    )
```

```python
import functools
import math

import jax
import jax.numpy as jnp
from jax import lax
from jax.experimental import pallas as pl
from jax.experimental.pallas import tpu as pltpu
from jax.sharding import PartitionSpec as P

D = 3072
HEADS = 12
HD = 128
BLK = 8
NBR = 9
CELLS = BLK * BLK


def extended_2(array, sides, width):
    for axis, dim in sides:
        size, length = (lax.axis_size(axis), array.shape[dim])
        up = [(i, (i + 1) % size) for i in range(size - 1)]
        down = [(j, i) for i, j in up]
        last = lax.slice_in_dim(array, length - width, length, axis=dim)
        first = lax.slice_in_dim(array, 0, width, axis=dim)
        before = lax.ppermute(last, axis, up)
        after = lax.ppermute(first, axis, down)
        array = jnp.concatenate([before, array, after], axis=dim)
    return array


def normalize(rows, shift_row, scale_row):
    widened = rows.astype(jnp.float32)
    average = jnp.mean(widened, axis=-1, keepdims=True)
    centred = widened - average
    spread = jnp.mean(centred * centred, axis=-1, keepdims=True)
    return (centred * lax.rsqrt(spread + 1e-06) * (1.0 + scale_row) + shift_row).astype(
        jnp.bfloat16
    )


def to_blocks(field):
    height, breadth, channels = field.shape
    shaped = field.reshape(height // BLK, BLK, breadth // BLK, BLK, channels)
    return shaped.transpose(0, 2, 1, 3, 4).reshape(
        height // BLK, breadth // BLK, BLK * BLK, channels
    )


def from_blocks(blocks):
    block_rows, block_cols, cells, channels = blocks.shape
    shaped = blocks.reshape(block_rows, block_cols, BLK, BLK, channels)
    return shaped.transpose(0, 2, 1, 3, 4).reshape(block_rows * BLK, block_cols * BLK, channels)


def attend_kernel(block_cols, codes_ref, counts_ref, live_ref, q_ref, kv_hbm, o_ref, kv_buf, sems):
    j = pl.program_id(0)
    n_blocks = pl.num_programs(0)
    ext_cols = block_cols + 2

    def copies(block, slot):
        out = []
        for l in range(NBR):
            code = jnp.clip(codes_ref[block * NBR + l], 0, NBR - 1)
            src = (block // block_cols + code // 3) * ext_cols + block % block_cols + code % 3
            out.append(
                pltpu.make_async_copy(
                    kv_hbm.at[src], kv_buf.at[slot, pl.ds(l * CELLS, CELLS)], sems.at[slot, l]
                )
            )
        return out

    @pl.when(j == 0)
    def _():
        for c in copies(j, 0):
            c.start()

    slot = j % 2

    @pl.when(j + 1 < n_blocks)
    def _():
        for c in copies(j + 1, 1 - slot):
            c.start()

    for c in copies(j, slot):
        c.wait()

    count = counts_ref[j]
    key_ids = lax.broadcasted_iota(jnp.int32, (CELLS, NBR * CELLS), 1)
    key_slot = key_ids // CELLS
    key_token = key_ids % CELLS
    limit = jnp.zeros((CELLS, NBR * CELLS), jnp.int32)
    for l in range(NBR):
        thr = jnp.where(l < count, live_ref[j * NBR + l], 0)
        limit = jnp.where(key_slot == l, thr, limit)
    live = key_token < limit
    width = HEADS * HD
    for h in range(HEADS):
        q = q_ref[0, :, h * HD:(h + 1) * HD]
        k = kv_buf[slot, :, h * HD:(h + 1) * HD]
        v = kv_buf[slot, :, width + h * HD:width + (h + 1) * HD]
        s = lax.dot_general(
            q, k, (((1,), (1,)), ((), ())), preferred_element_type=jnp.float32
        ) * (1.0 / math.sqrt(HD))
        s = jnp.where(live, s, -jnp.inf)
        m = jnp.max(s, axis=-1, keepdims=True)
        e = jnp.exp(s - m)
        p = (e / jnp.sum(e, axis=-1, keepdims=True)).astype(jnp.bfloat16)
        o = jnp.dot(p, v, preferred_element_type=jnp.float32)
        o_ref[0, :, h * HD:(h + 1) * HD] = o.astype(o_ref.dtype)


def local_attention(q_blocks, kv_blocks, codes, counts, live_count, block_cols):
    n_blocks = q_blocks.shape[0]
    width = q_blocks.shape[-1]
    grid_spec = pltpu.PrefetchScalarGridSpec(
        num_scalar_prefetch=3,
        grid=(n_blocks,),
        in_specs=[
            pl.BlockSpec((1, CELLS, width), lambda j, *_: (j, 0, 0)),
            pl.BlockSpec(memory_space=pl.ANY),
        ],
        out_specs=pl.BlockSpec((1, CELLS, width), lambda j, *_: (j, 0, 0)),
        scratch_shapes=[
            pltpu.VMEM((2, NBR * CELLS, 2 * width), jnp.bfloat16),
            pltpu.SemaphoreType.DMA((2, NBR)),
        ],
    )
    return pl.pallas_call(
        functools.partial(attend_kernel, block_cols),
        grid_spec=grid_spec,
        out_shape=jax.ShapeDtypeStruct(q_blocks.shape, jnp.bfloat16),
        compiler_params=pltpu.CompilerParams(dimension_semantics=("arbitrary",)),
    )(codes.reshape(-1), counts.reshape(-1), live_count.reshape(-1), q_blocks, kv_blocks)


def body(tokens, mod_shift, mod_scale, qkv_weight, block_codes, block_counts, valid_tokens):
    tile_rows = tokens.shape[1]
    tile_cols = tokens.shape[2]
    width = HEADS * HD
    rows_axis = lax.axis_size("gy")
    to_next = [(i, i + 1) for i in range(rows_axis - 1)]
    to_prev = [(i + 1, i) for i in range(rows_axis - 1)]
    above = lax.ppermute(tokens[0], "gy", to_next)
    below = lax.ppermute(tokens[0], "gy", to_prev)
    weight = lax.all_gather(qkv_weight, ("gx", "wa"), axis=1, tiled=True)
    flat_rows = normalize(tokens[0], mod_shift[0], mod_scale[0]).reshape(tile_rows * tile_cols, D)
    qkv = jnp.dot(flat_rows, weight, preferred_element_type=jnp.float32).astype(jnp.bfloat16)
    halo_rows = normalize(
        jnp.concatenate([above, below], axis=0), mod_shift[0], mod_scale[0]
    ).reshape(2 * tile_rows * tile_cols, D)
    halo_kv = jnp.dot(
        halo_rows, weight[:, width:], preferred_element_type=jnp.float32
    ).astype(jnp.bfloat16).reshape(2 * tile_rows, tile_cols, 2 * width)
    qkv_grid = qkv.reshape(tile_rows, tile_cols, 3 * width)
    extended = jnp.concatenate(
        [halo_kv[:tile_rows], qkv_grid[:, :, width:], halo_kv[tile_rows:]], axis=0
    )
    extended = extended_2(extended, (("gx", 1),), BLK)
    block_rows = tile_rows // BLK
    block_cols = tile_cols // BLK
    queries = to_blocks(qkv_grid[:, :, :width])
    key_blocks = to_blocks(extended)
    row_ids = jnp.arange(block_rows, dtype=jnp.int32)[:, None, None]
    col_ids = jnp.arange(block_cols, dtype=jnp.int32)[None, :, None]
    row_step = block_codes // 3 - 1
    col_step = block_codes % 3 - 1
    global_row = jnp.clip(
        lax.axis_index("gy") * block_rows + row_ids + row_step, 0, valid_tokens.shape[0] - 1
    )
    global_col = jnp.clip(
        lax.axis_index("gx") * block_cols + col_ids + col_step, 0, valid_tokens.shape[1] - 1
    )
    live_count = valid_tokens[global_row, global_col]
    number = block_rows * block_cols
    result = local_attention(
        queries.reshape(number, CELLS, width),
        key_blocks.reshape(-1, CELLS, 2 * width),
        block_codes.reshape(number, NBR),
        block_counts.reshape(number),
        live_count.reshape(number, NBR),
        block_cols,
    )
    return from_blocks(result.reshape(block_rows, block_cols, CELLS, width))[None]


def solution(mesh):
    return jax.shard_map(
        body,
        mesh=mesh,
        in_specs=(
            P("wa", "gy", "gx", None),
            P("wa", None),
            P("wa", None),
            P(None, ("gx", "wa")),
            P("gy", "gx", None),
            P("gy", "gx"),
            P(),
        ),
        out_specs=P("wa", "gy", "gx", None),
        check_vma=False,
    )
```

```python
import functools
import math

import jax
import jax.numpy as jnp
from jax import lax
from jax.experimental import pallas as pl
from jax.experimental.pallas import tpu as pltpu
from jax.sharding import PartitionSpec as P

D = 3072
HEADS = 12
HD = 128
BLK = 8
NBR = 9
CELLS = BLK * BLK


def extended_2(array, sides, width):
    for axis, dim in sides:
        size, length = (lax.axis_size(axis), array.shape[dim])
        up = [(i, (i + 1) % size) for i in range(size - 1)]
        down = [(j, i) for i, j in up]
        last = lax.slice_in_dim(array, length - width, length, axis=dim)
        first = lax.slice_in_dim(array, 0, width, axis=dim)
        before = lax.ppermute(last, axis, up)
        after = lax.ppermute(first, axis, down)
        array = jnp.concatenate([before, array, after], axis=dim)
    return array


def normalize(rows, shift_row, scale_row):
    widened = rows.astype(jnp.float32)
    average = jnp.mean(widened, axis=-1, keepdims=True)
    centred = widened - average
    spread = jnp.mean(centred * centred, axis=-1, keepdims=True)
    return (centred * lax.rsqrt(spread + 1e-06) * (1.0 + scale_row) + shift_row).astype(
        jnp.bfloat16
    )


def to_blocks(field):
    height, breadth, channels = field.shape
    shaped = field.reshape(height // BLK, BLK, breadth // BLK, BLK, channels)
    return shaped.transpose(0, 2, 1, 3, 4).reshape(
        height // BLK, breadth // BLK, BLK * BLK, channels
    )


def from_blocks(blocks):
    block_rows, block_cols, cells, channels = blocks.shape
    shaped = blocks.reshape(block_rows, block_cols, BLK, BLK, channels)
    return shaped.transpose(0, 2, 1, 3, 4).reshape(block_rows * BLK, block_cols * BLK, channels)


def attend_kernel(block_cols, codes_ref, counts_ref, live_ref, q_ref, kv_hbm, o_ref, kv_buf, sems):
    j = pl.program_id(0)
    n_blocks = pl.num_programs(0)
    ext_cols = block_cols + 2

    def copies(block, slot):
        out = []
        for l in range(NBR):
            code = jnp.clip(codes_ref[block * NBR + l], 0, NBR - 1)
            src = (block // block_cols + code // 3) * ext_cols + block % block_cols + code % 3
            out.append(
                pltpu.make_async_copy(
                    kv_hbm.at[src], kv_buf.at[slot, pl.ds(l * CELLS, CELLS)], sems.at[slot, l]
                )
            )
        return out

    @pl.when(j == 0)
    def _():
        for c in copies(j, 0):
            c.start()

    slot = j % 2

    @pl.when(j + 1 < n_blocks)
    def _():
        for c in copies(j + 1, 1 - slot):
            c.start()

    for c in copies(j, slot):
        c.wait()

    count = counts_ref[j]
    key_ids = lax.broadcasted_iota(jnp.int32, (CELLS, NBR * CELLS), 1)
    key_slot = key_ids // CELLS
    key_token = key_ids % CELLS
    limit = jnp.zeros((CELLS, NBR * CELLS), jnp.int32)
    for l in range(NBR):
        thr = jnp.where(l < count, live_ref[j * NBR + l], 0)
        limit = jnp.where(key_slot == l, thr, limit)
    live = key_token < limit
    width = HEADS * HD
    for h in range(HEADS):
        q = q_ref[0, :, h * HD:(h + 1) * HD]
        k = kv_buf[slot, :, h * HD:(h + 1) * HD]
        v = kv_buf[slot, :, width + h * HD:width + (h + 1) * HD]
        s = lax.dot_general(
            q, k, (((1,), (1,)), ((), ())), preferred_element_type=jnp.float32
        ) * (1.0 / math.sqrt(HD))
        s = jnp.where(live, s, -jnp.inf)
        m = jnp.max(s, axis=-1, keepdims=True)
        e = jnp.exp(s - m)
        p = (e / jnp.sum(e, axis=-1, keepdims=True)).astype(jnp.bfloat16)
        o = jnp.dot(p, v, preferred_element_type=jnp.float32)
        o_ref[0, :, h * HD:(h + 1) * HD] = o.astype(o_ref.dtype)


def local_attention(q_blocks, kv_blocks, codes, counts, live_count, block_cols):
    n_blocks = q_blocks.shape[0]
    width = q_blocks.shape[-1]
    grid_spec = pltpu.PrefetchScalarGridSpec(
        num_scalar_prefetch=3,
        grid=(n_blocks,),
        in_specs=[
            pl.BlockSpec((1, CELLS, width), lambda j, *_: (j, 0, 0)),
            pl.BlockSpec(memory_space=pl.ANY),
        ],
        out_specs=pl.BlockSpec((1, CELLS, width), lambda j, *_: (j, 0, 0)),
        scratch_shapes=[
            pltpu.VMEM((2, NBR * CELLS, 2 * width), jnp.bfloat16),
            pltpu.SemaphoreType.DMA((2, NBR)),
        ],
    )
    return pl.pallas_call(
        functools.partial(attend_kernel, block_cols),
        grid_spec=grid_spec,
        out_shape=jax.ShapeDtypeStruct(q_blocks.shape, jnp.bfloat16),
        compiler_params=pltpu.CompilerParams(dimension_semantics=("arbitrary",)),
    )(codes.reshape(-1), counts.reshape(-1), live_count.reshape(-1), q_blocks, kv_blocks)


def body(tokens, mod_shift, mod_scale, qkv_weight, block_codes, block_counts, valid_tokens):
    tile_rows = tokens.shape[1]
    tile_cols = tokens.shape[2]
    width = HEADS * HD
    group = lax.axis_size("gx")
    me = lax.axis_index("gx")
    tile = tokens[0]
    received = [tile] + [
        lax.ppermute(tile, "gx", [(i, (i + d) % group) for i in range(group)])
        for d in range(1, group)
    ]
    weight_block = lax.all_gather(qkv_weight, "wa", axis=1, tiled=True)
    strip = normalize(jnp.stack(received), mod_shift[0], mod_scale[0]).reshape(
        group, tile_rows * tile_cols, D
    )
    partial = jnp.dot(
        strip.reshape(group * tile_rows * tile_cols, D),
        weight_block,
        preferred_element_type=jnp.float32,
    ).astype(jnp.bfloat16).reshape(group, tile_rows * tile_cols, -1)
    returned = [partial[0]] + [
        lax.ppermute(partial[d], "gx", [(i, (i - d) % group) for i in range(group)])
        for d in range(1, group)
    ]
    doubled = jnp.stack(returned + returned)
    ordered = lax.dynamic_slice_in_dim(doubled, group - me, group, axis=0)
    qkv = ordered.transpose(1, 0, 2).reshape(tile_rows * tile_cols, 3 * width)
    qkv_grid = qkv.reshape(tile_rows, tile_cols, 3 * width)
    extended = extended_2(qkv_grid[:, :, width:], (("gy", 0), ("gx", 1)), BLK)
    block_rows = tile_rows // BLK
    block_cols = tile_cols // BLK
    queries = to_blocks(qkv_grid[:, :, :width])
    key_blocks = to_blocks(extended)
    row_ids = jnp.arange(block_rows, dtype=jnp.int32)[:, None, None]
    col_ids = jnp.arange(block_cols, dtype=jnp.int32)[None, :, None]
    row_step = block_codes // 3 - 1
    col_step = block_codes % 3 - 1
    global_row = jnp.clip(
        lax.axis_index("gy") * block_rows + row_ids + row_step, 0, valid_tokens.shape[0] - 1
    )
    global_col = jnp.clip(
        lax.axis_index("gx") * block_cols + col_ids + col_step, 0, valid_tokens.shape[1] - 1
    )
    live_count = valid_tokens[global_row, global_col]
    number = block_rows * block_cols
    result = local_attention(
        queries.reshape(number, CELLS, width),
        key_blocks.reshape(-1, CELLS, 2 * width),
        block_codes.reshape(number, NBR),
        block_counts.reshape(number),
        live_count.reshape(number, NBR),
        block_cols,
    )
    return from_blocks(result.reshape(block_rows, block_cols, CELLS, width))[None]


def solution(mesh):
    return jax.shard_map(
        body,
        mesh=mesh,
        in_specs=(
            P("wa", "gy", "gx", None),
            P("wa", None),
            P("wa", None),
            P(None, ("gx", "wa")),
            P("gy", "gx", None),
            P("gy", "gx"),
            P(),
        ),
        out_specs=P("wa", "gy", "gx", None),
        check_vma=False,
    )
```

```python
import functools
import math

import jax
import jax.numpy as jnp
from jax import lax
from jax.experimental import pallas as pl
from jax.experimental.pallas import tpu as pltpu
from jax.sharding import PartitionSpec as P

D = 3072
HEADS = 12
HD = 128
BLK = 8
NBR = 9
CELLS = BLK * BLK


def extended_2(array, sides, width):
    for axis, dim in sides:
        size, length = (lax.axis_size(axis), array.shape[dim])
        up = [(i, (i + 1) % size) for i in range(size - 1)]
        down = [(j, i) for i, j in up]
        last = lax.slice_in_dim(array, length - width, length, axis=dim)
        first = lax.slice_in_dim(array, 0, width, axis=dim)
        before = lax.ppermute(last, axis, up)
        after = lax.ppermute(first, axis, down)
        array = jnp.concatenate([before, array, after], axis=dim)
    return array


def normalize(rows, shift_row, scale_row):
    widened = rows.astype(jnp.float32)
    average = jnp.mean(widened, axis=-1, keepdims=True)
    centred = widened - average
    spread = jnp.mean(centred * centred, axis=-1, keepdims=True)
    return (centred * lax.rsqrt(spread + 1e-06) * (1.0 + scale_row) + shift_row).astype(
        jnp.bfloat16
    )


def to_blocks(field):
    height, breadth, channels = field.shape
    shaped = field.reshape(height // BLK, BLK, breadth // BLK, BLK, channels)
    return shaped.transpose(0, 2, 1, 3, 4).reshape(
        height // BLK, breadth // BLK, BLK * BLK, channels
    )


def from_blocks(blocks):
    block_rows, block_cols, cells, channels = blocks.shape
    shaped = blocks.reshape(block_rows, block_cols, BLK, BLK, channels)
    return shaped.transpose(0, 2, 1, 3, 4).reshape(block_rows * BLK, block_cols * BLK, channels)


def attend_kernel(block_cols, codes_ref, counts_ref, live_ref, q_ref, kv_hbm, o_ref, kv_buf, sems):
    j = pl.program_id(0)
    n_blocks = pl.num_programs(0)
    ext_cols = block_cols + 2

    def copies(block, slot):
        out = []
        for l in range(NBR):
            code = jnp.clip(codes_ref[block * NBR + l], 0, NBR - 1)
            src = (block // block_cols + code // 3) * ext_cols + block % block_cols + code % 3
            out.append(
                pltpu.make_async_copy(
                    kv_hbm.at[src], kv_buf.at[slot, pl.ds(l * CELLS, CELLS)], sems.at[slot, l]
                )
            )
        return out

    @pl.when(j == 0)
    def _():
        for c in copies(j, 0):
            c.start()

    slot = j % 2

    @pl.when(j + 1 < n_blocks)
    def _():
        for c in copies(j + 1, 1 - slot):
            c.start()

    for c in copies(j, slot):
        c.wait()

    count = counts_ref[j]
    key_ids = lax.broadcasted_iota(jnp.int32, (CELLS, NBR * CELLS), 1)
    key_slot = key_ids // CELLS
    key_token = key_ids % CELLS
    limit = jnp.zeros((CELLS, NBR * CELLS), jnp.int32)
    for l in range(NBR):
        thr = jnp.where(l < count, live_ref[j * NBR + l], 0)
        limit = jnp.where(key_slot == l, thr, limit)
    live = key_token < limit
    width = HEADS * HD
    for h in range(HEADS):
        q = q_ref[0, :, h * HD:(h + 1) * HD]
        k = kv_buf[slot, :, h * HD:(h + 1) * HD]
        v = kv_buf[slot, :, width + h * HD:width + (h + 1) * HD]
        s = lax.dot_general(
            q, k, (((1,), (1,)), ((), ())), preferred_element_type=jnp.float32
        ) * (1.0 / math.sqrt(HD))
        s = jnp.where(live, s, -jnp.inf)
        m = jnp.max(s, axis=-1, keepdims=True)
        e = jnp.exp(s - m)
        p = (e / jnp.sum(e, axis=-1, keepdims=True)).astype(jnp.bfloat16)
        o = jnp.dot(p, v, preferred_element_type=jnp.float32)
        o_ref[0, :, h * HD:(h + 1) * HD] = o.astype(o_ref.dtype)


def local_attention(q_blocks, kv_blocks, codes, counts, live_count, block_cols):
    n_blocks = q_blocks.shape[0]
    width = q_blocks.shape[-1]
    grid_spec = pltpu.PrefetchScalarGridSpec(
        num_scalar_prefetch=3,
        grid=(n_blocks,),
        in_specs=[
            pl.BlockSpec((1, CELLS, width), lambda j, *_: (j, 0, 0)),
            pl.BlockSpec(memory_space=pl.ANY),
        ],
        out_specs=pl.BlockSpec((1, CELLS, width), lambda j, *_: (j, 0, 0)),
        scratch_shapes=[
            pltpu.VMEM((2, NBR * CELLS, 2 * width), jnp.bfloat16),
            pltpu.SemaphoreType.DMA((2, NBR)),
        ],
    )
    return pl.pallas_call(
        functools.partial(attend_kernel, block_cols),
        grid_spec=grid_spec,
        out_shape=jax.ShapeDtypeStruct(q_blocks.shape, jnp.bfloat16),
        compiler_params=pltpu.CompilerParams(dimension_semantics=("arbitrary",)),
    )(codes.reshape(-1), counts.reshape(-1), live_count.reshape(-1), q_blocks, kv_blocks)


def body(tokens, mod_shift, mod_scale, qkv_weight, block_codes, block_counts, valid_tokens):
    tile_rows = tokens.shape[1]
    tile_cols = tokens.shape[2]
    width = HEADS * HD
    group = lax.axis_size("gx")
    me = lax.axis_index("gx")
    tile = tokens[0]
    received = [tile] + [
        lax.ppermute(tile, "gx", [(i, (i + d) % group) for i in range(group)])
        for d in range(1, group)
    ]
    weight_block = lax.all_gather(qkv_weight, "wa", axis=1, tiled=True)
    strip = normalize(jnp.stack(received), mod_shift[0], mod_scale[0]).reshape(
        group, tile_rows * tile_cols, D
    )
    partial = jnp.dot(
        strip.reshape(group * tile_rows * tile_cols, D),
        weight_block,
        preferred_element_type=jnp.float32,
    ).astype(jnp.bfloat16).reshape(group, tile_rows * tile_cols, -1)
    returned = [partial[0]] + [
        lax.ppermute(partial[d], "gx", [(i, (i - d) % group) for i in range(group)])
        for d in range(1, group)
    ]
    rows_axis = lax.axis_size("gy")
    block = partial.shape[-1]
    senders = [g for g in range(group) if (g + 1) * block > width]

    def neighbour_rows(step):
        chunks = []
        for d in range(group):
            pairs = [
                (r * group + g, (r + step) * group + (g - d) % group)
                for r in range(rows_axis)
                if 0 <= r + step < rows_axis
                for g in senders
            ]
            chunks.append(lax.ppermute(partial[d], ("gy", "gx"), pairs))
        return assemble(chunks)[:, :, width:]

    def assemble(chunks):
        doubled = jnp.stack(chunks + chunks)
        ordered = lax.dynamic_slice_in_dim(doubled, group - me, group, axis=0)
        return ordered.transpose(1, 0, 2).reshape(tile_rows, tile_cols, 3 * width)

    above = neighbour_rows(1)
    below = neighbour_rows(-1)
    qkv_grid = assemble(returned)
    extended = jnp.concatenate([above, qkv_grid[:, :, width:], below], axis=0)
    extended = extended_2(extended, (("gx", 1),), BLK)
    block_rows = tile_rows // BLK
    block_cols = tile_cols // BLK
    queries = to_blocks(qkv_grid[:, :, :width])
    key_blocks = to_blocks(extended)
    row_ids = jnp.arange(block_rows, dtype=jnp.int32)[:, None, None]
    col_ids = jnp.arange(block_cols, dtype=jnp.int32)[None, :, None]
    row_step = block_codes // 3 - 1
    col_step = block_codes % 3 - 1
    global_row = jnp.clip(
        lax.axis_index("gy") * block_rows + row_ids + row_step, 0, valid_tokens.shape[0] - 1
    )
    global_col = jnp.clip(
        lax.axis_index("gx") * block_cols + col_ids + col_step, 0, valid_tokens.shape[1] - 1
    )
    live_count = valid_tokens[global_row, global_col]
    number = block_rows * block_cols
    result = local_attention(
        queries.reshape(number, CELLS, width),
        key_blocks.reshape(-1, CELLS, 2 * width),
        block_codes.reshape(number, NBR),
        block_counts.reshape(number),
        live_count.reshape(number, NBR),
        block_cols,
    )
    return from_blocks(result.reshape(block_rows, block_cols, CELLS, width))[None]


def solution(mesh):
    return jax.shard_map(
        body,
        mesh=mesh,
        in_specs=(
            P("wa", "gy", "gx", None),
            P("wa", None),
            P("wa", None),
            P(None, ("gx", "wa")),
            P("gy", "gx", None),
            P("gy", "gx"),
            P(),
        ),
        out_specs=P("wa", "gy", "gx", None),
        check_vma=False,
    )
```

```python
import functools
import math

import jax
import jax.numpy as jnp
from jax import lax
from jax.experimental import pallas as pl
from jax.experimental.pallas import tpu as pltpu
from jax.sharding import PartitionSpec as P

D = 3072
HEADS = 12
HD = 128
BLK = 8
NBR = 9
CELLS = BLK * BLK


def extended_2(array, sides, width):
    for axis, dim in sides:
        size, length = (lax.axis_size(axis), array.shape[dim])
        up = [(i, (i + 1) % size) for i in range(size - 1)]
        down = [(j, i) for i, j in up]
        last = lax.slice_in_dim(array, length - width, length, axis=dim)
        first = lax.slice_in_dim(array, 0, width, axis=dim)
        before = lax.ppermute(last, axis, up)
        after = lax.ppermute(first, axis, down)
        array = jnp.concatenate([before, array, after], axis=dim)
    return array


def normalize(rows, shift_row, scale_row):
    widened = rows.astype(jnp.float32)
    average = jnp.mean(widened, axis=-1, keepdims=True)
    centred = widened - average
    spread = jnp.mean(centred * centred, axis=-1, keepdims=True)
    return (centred * lax.rsqrt(spread + 1e-06) * (1.0 + scale_row) + shift_row).astype(
        jnp.bfloat16
    )


def to_blocks(field):
    height, breadth, channels = field.shape
    shaped = field.reshape(height // BLK, BLK, breadth // BLK, BLK, channels)
    return shaped.transpose(0, 2, 1, 3, 4).reshape(
        height // BLK, breadth // BLK, BLK * BLK, channels
    )


def from_blocks(blocks):
    block_rows, block_cols, cells, channels = blocks.shape
    shaped = blocks.reshape(block_rows, block_cols, BLK, BLK, channels)
    return shaped.transpose(0, 2, 1, 3, 4).reshape(block_rows * BLK, block_cols * BLK, channels)


def attend_kernel(block_cols, codes_ref, counts_ref, live_ref, q_ref, kv_hbm, o_ref, kv_buf, sems):
    j = pl.program_id(0)
    n_blocks = pl.num_programs(0)
    ext_cols = block_cols + 2

    def copies(block, slot):
        out = []
        for l in range(NBR):
            code = jnp.clip(codes_ref[block * NBR + l], 0, NBR - 1)
            src = (block // block_cols + code // 3) * ext_cols + block % block_cols + code % 3
            out.append(
                pltpu.make_async_copy(
                    kv_hbm.at[src], kv_buf.at[slot, pl.ds(l * CELLS, CELLS)], sems.at[slot, l]
                )
            )
        return out

    @pl.when(j == 0)
    def _():
        for c in copies(j, 0):
            c.start()

    slot = j % 2

    @pl.when(j + 1 < n_blocks)
    def _():
        for c in copies(j + 1, 1 - slot):
            c.start()

    for c in copies(j, slot):
        c.wait()

    count = counts_ref[j]
    key_ids = lax.broadcasted_iota(jnp.int32, (CELLS, NBR * CELLS), 1)
    key_slot = key_ids // CELLS
    key_token = key_ids % CELLS
    limit = jnp.zeros((CELLS, NBR * CELLS), jnp.int32)
    for l in range(NBR):
        thr = jnp.where(l < count, live_ref[j * NBR + l], 0)
        limit = jnp.where(key_slot == l, thr, limit)
    live = key_token < limit
    width = HEADS * HD
    for h in range(HEADS):
        q = q_ref[0, :, h * HD:(h + 1) * HD]
        k = kv_buf[slot, :, h * HD:(h + 1) * HD]
        v = kv_buf[slot, :, width + h * HD:width + (h + 1) * HD]
        s = lax.dot_general(
            q, k, (((1,), (1,)), ((), ())), preferred_element_type=jnp.float32
        ) * (1.0 / math.sqrt(HD))
        s = jnp.where(live, s, -jnp.inf)
        m = jnp.max(s, axis=-1, keepdims=True)
        e = jnp.exp(s - m)
        p = (e / jnp.sum(e, axis=-1, keepdims=True)).astype(jnp.bfloat16)
        o = jnp.dot(p, v, preferred_element_type=jnp.float32)
        o_ref[0, :, h * HD:(h + 1) * HD] = o.astype(o_ref.dtype)


def local_attention(q_blocks, kv_blocks, codes, counts, live_count, block_cols):
    n_blocks = q_blocks.shape[0]
    width = q_blocks.shape[-1]
    grid_spec = pltpu.PrefetchScalarGridSpec(
        num_scalar_prefetch=3,
        grid=(n_blocks,),
        in_specs=[
            pl.BlockSpec((1, CELLS, width), lambda j, *_: (j, 0, 0)),
            pl.BlockSpec(memory_space=pl.ANY),
        ],
        out_specs=pl.BlockSpec((1, CELLS, width), lambda j, *_: (j, 0, 0)),
        scratch_shapes=[
            pltpu.VMEM((2, NBR * CELLS, 2 * width), jnp.bfloat16),
            pltpu.SemaphoreType.DMA((2, NBR)),
        ],
    )
    return pl.pallas_call(
        functools.partial(attend_kernel, block_cols),
        grid_spec=grid_spec,
        out_shape=jax.ShapeDtypeStruct(q_blocks.shape, jnp.bfloat16),
        compiler_params=pltpu.CompilerParams(dimension_semantics=("arbitrary",)),
    )(codes.reshape(-1), counts.reshape(-1), live_count.reshape(-1), q_blocks, kv_blocks)


def body(tokens, mod_shift, mod_scale, qkv_weight, block_codes, block_counts, valid_tokens):
    tile_rows = tokens.shape[1]
    tile_cols = tokens.shape[2]
    width = HEADS * HD
    group = lax.axis_size("gx")
    me = lax.axis_index("gx")
    tile = tokens[0]
    received = [tile] + [
        lax.ppermute(tile, "gx", [(i, (i + d) % group) for i in range(group)])
        for d in range(1, group)
    ]
    weight_block = lax.all_gather(qkv_weight, "wa", axis=1, tiled=True)
    strip = normalize(jnp.stack(received), mod_shift[0], mod_scale[0]).reshape(
        group, tile_rows * tile_cols, D
    )
    partial = jnp.dot(
        strip.reshape(group * tile_rows * tile_cols, D),
        weight_block,
        preferred_element_type=jnp.float32,
    ).astype(jnp.bfloat16).reshape(group, tile_rows * tile_cols, -1)
    returned = [partial[0]] + [
        lax.ppermute(partial[d], "gx", [(i, (i - d) % group) for i in range(group)])
        for d in range(1, group)
    ]
    rows_axis = lax.axis_size("gy")
    block = partial.shape[-1]
    senders = [g for g in range(group) if (g + 1) * block > width]

    def neighbour_rows(step):
        chunks = []
        for d in range(group):
            pairs = [
                (r * group + g, (r + step) * group + (g - d) % group)
                for r in range(rows_axis)
                if 0 <= r + step < rows_axis
                for g in senders
            ]
            chunks.append(lax.ppermute(partial[d], ("gy", "gx"), pairs))
        return assemble(chunks)[:, :, width:]

    def assemble(chunks):
        blocks = []
        for b in range(group):
            pick = (b - me) % group
            chosen = chunks[0]
            for d in range(1, group):
                chosen = jnp.where(pick == d, chunks[d], chosen)
            blocks.append(chosen)
        return jnp.concatenate(blocks, axis=1).reshape(tile_rows, tile_cols, 3 * width)

    above = neighbour_rows(1)
    below = neighbour_rows(-1)
    qkv_grid = assemble(returned)
    extended = jnp.concatenate([above, qkv_grid[:, :, width:], below], axis=0)
    extended = extended_2(extended, (("gx", 1),), BLK)
    block_rows = tile_rows // BLK
    block_cols = tile_cols // BLK
    queries = to_blocks(qkv_grid[:, :, :width])
    key_blocks = to_blocks(extended)
    row_ids = jnp.arange(block_rows, dtype=jnp.int32)[:, None, None]
    col_ids = jnp.arange(block_cols, dtype=jnp.int32)[None, :, None]
    row_step = block_codes // 3 - 1
    col_step = block_codes % 3 - 1
    global_row = jnp.clip(
        lax.axis_index("gy") * block_rows + row_ids + row_step, 0, valid_tokens.shape[0] - 1
    )
    global_col = jnp.clip(
        lax.axis_index("gx") * block_cols + col_ids + col_step, 0, valid_tokens.shape[1] - 1
    )
    live_count = valid_tokens[global_row, global_col]
    number = block_rows * block_cols
    result = local_attention(
        queries.reshape(number, CELLS, width),
        key_blocks.reshape(-1, CELLS, 2 * width),
        block_codes.reshape(number, NBR),
        block_counts.reshape(number),
        live_count.reshape(number, NBR),
        block_cols,
    )
    return from_blocks(result.reshape(block_rows, block_cols, CELLS, width))[None]


def solution(mesh):
    return jax.shard_map(
        body,
        mesh=mesh,
        in_specs=(
            P("wa", "gy", "gx", None),
            P("wa", None),
            P("wa", None),
            P(None, ("gx", "wa")),
            P("gy", "gx", None),
            P("gy", "gx"),
            P(),
        ),
        out_specs=P("wa", "gy", "gx", None),
        check_vma=False,
    )
```

```python
import functools
import math

import jax
import jax.numpy as jnp
from jax import lax
from jax.experimental import pallas as pl
from jax.experimental.pallas import tpu as pltpu
from jax.sharding import PartitionSpec as P

D = 3072
HEADS = 12
HD = 128
BLK = 8
NBR = 9
CELLS = BLK * BLK


def extended_2(array, sides, width):
    for axis, dim in sides:
        size, length = (lax.axis_size(axis), array.shape[dim])
        up = [(i, (i + 1) % size) for i in range(size - 1)]
        down = [(j, i) for i, j in up]
        last = lax.slice_in_dim(array, length - width, length, axis=dim)
        first = lax.slice_in_dim(array, 0, width, axis=dim)
        before = lax.ppermute(last, axis, up)
        after = lax.ppermute(first, axis, down)
        array = jnp.concatenate([before, array, after], axis=dim)
    return array


def normalize(rows, shift_row, scale_row):
    widened = rows.astype(jnp.float32)
    average = jnp.mean(widened, axis=-1, keepdims=True)
    centred = widened - average
    spread = jnp.mean(centred * centred, axis=-1, keepdims=True)
    return (centred * lax.rsqrt(spread + 1e-06) * (1.0 + scale_row) + shift_row).astype(
        jnp.bfloat16
    )


def to_blocks(field):
    height, breadth, channels = field.shape
    shaped = field.reshape(height // BLK, BLK, breadth // BLK, BLK, channels)
    return shaped.transpose(0, 2, 1, 3, 4).reshape(
        height // BLK, breadth // BLK, BLK * BLK, channels
    )


def from_blocks(blocks):
    block_rows, block_cols, cells, channels = blocks.shape
    shaped = blocks.reshape(block_rows, block_cols, BLK, BLK, channels)
    return shaped.transpose(0, 2, 1, 3, 4).reshape(block_rows * BLK, block_cols * BLK, channels)


def attend_kernel(block_cols, codes_ref, counts_ref, live_ref, q_ref, kv_hbm, o_ref, kv_buf, sems):
    j = pl.program_id(0)
    n_blocks = pl.num_programs(0)
    ext_cols = block_cols + 2

    def copies(block, slot):
        out = []
        for l in range(NBR):
            code = jnp.clip(codes_ref[block * NBR + l], 0, NBR - 1)
            src = (block // block_cols + code // 3) * ext_cols + block % block_cols + code % 3
            out.append(
                pltpu.make_async_copy(
                    kv_hbm.at[src], kv_buf.at[slot, pl.ds(l * CELLS, CELLS)], sems.at[slot, l]
                )
            )
        return out

    @pl.when(j == 0)
    def _():
        for c in copies(j, 0):
            c.start()

    slot = j % 2

    @pl.when(j + 1 < n_blocks)
    def _():
        for c in copies(j + 1, 1 - slot):
            c.start()

    for c in copies(j, slot):
        c.wait()

    count = counts_ref[j]
    key_ids = lax.broadcasted_iota(jnp.int32, (CELLS, NBR * CELLS), 1)
    key_slot = key_ids // CELLS
    key_token = key_ids % CELLS
    limit = jnp.zeros((CELLS, NBR * CELLS), jnp.int32)
    for l in range(NBR):
        thr = jnp.where(l < count, live_ref[j * NBR + l], 0)
        limit = jnp.where(key_slot == l, thr, limit)
    live = key_token < limit
    width = HEADS * HD
    for h in range(HEADS):
        q = q_ref[0, :, h * HD:(h + 1) * HD]
        k = kv_buf[slot, :, h * HD:(h + 1) * HD]
        v = kv_buf[slot, :, width + h * HD:width + (h + 1) * HD]
        s = lax.dot_general(
            q, k, (((1,), (1,)), ((), ())), preferred_element_type=jnp.float32
        ) * (1.0 / math.sqrt(HD))
        s = jnp.where(live, s, -jnp.inf)
        m = jnp.max(s, axis=-1, keepdims=True)
        e = jnp.exp(s - m)
        p = (e / jnp.sum(e, axis=-1, keepdims=True)).astype(jnp.bfloat16)
        o = jnp.dot(p, v, preferred_element_type=jnp.float32)
        o_ref[0, :, h * HD:(h + 1) * HD] = o.astype(o_ref.dtype)


def local_attention(q_blocks, kv_blocks, codes, counts, live_count, block_cols):
    n_blocks = q_blocks.shape[0]
    width = q_blocks.shape[-1]
    grid_spec = pltpu.PrefetchScalarGridSpec(
        num_scalar_prefetch=3,
        grid=(n_blocks,),
        in_specs=[
            pl.BlockSpec((1, CELLS, width), lambda j, *_: (j, 0, 0)),
            pl.BlockSpec(memory_space=pl.ANY),
        ],
        out_specs=pl.BlockSpec((1, CELLS, width), lambda j, *_: (j, 0, 0)),
        scratch_shapes=[
            pltpu.VMEM((2, NBR * CELLS, 2 * width), jnp.bfloat16),
            pltpu.SemaphoreType.DMA((2, NBR)),
        ],
    )
    return pl.pallas_call(
        functools.partial(attend_kernel, block_cols),
        grid_spec=grid_spec,
        out_shape=jax.ShapeDtypeStruct(q_blocks.shape, jnp.bfloat16),
        compiler_params=pltpu.CompilerParams(dimension_semantics=("arbitrary",)),
    )(codes.reshape(-1), counts.reshape(-1), live_count.reshape(-1), q_blocks, kv_blocks)


def body(tokens, mod_shift, mod_scale, qkv_weight, block_codes, block_counts, valid_tokens):
    tile_rows = tokens.shape[1]
    tile_cols = tokens.shape[2]
    width = HEADS * HD
    group = lax.axis_size("gx")
    me = lax.axis_index("gx")
    tile = tokens[0]
    received = [tile] + [
        lax.ppermute(tile, "gx", [(i, (i + d) % group) for i in range(group)])
        for d in range(1, group)
    ]
    weight_block = lax.all_gather(qkv_weight, "wa", axis=1, tiled=True)
    strip = normalize(jnp.stack(received), mod_shift[0], mod_scale[0]).reshape(
        group, tile_rows * tile_cols, D
    )
    partial = [
        jnp.dot(strip[d], weight_block, preferred_element_type=jnp.float32).astype(jnp.bfloat16)
        for d in range(group)
    ]
    returned = [partial[0]] + [
        lax.ppermute(partial[d], "gx", [(i, (i - d) % group) for i in range(group)])
        for d in range(1, group)
    ]
    rows_axis = lax.axis_size("gy")
    block = partial[0].shape[-1]
    senders = [g for g in range(group) if (g + 1) * block > width]

    def neighbour_rows(step):
        chunks = []
        for d in range(group):
            pairs = [
                (r * group + g, (r + step) * group + (g - d) % group)
                for r in range(rows_axis)
                if 0 <= r + step < rows_axis
                for g in senders
            ]
            chunks.append(lax.ppermute(partial[d], ("gy", "gx"), pairs))
        return assemble(chunks)[:, :, width:]

    def assemble(chunks):
        blocks = []
        for b in range(group):
            pick = (b - me) % group
            chosen = chunks[0]
            for d in range(1, group):
                chosen = jnp.where(pick == d, chunks[d], chosen)
            blocks.append(chosen)
        return jnp.concatenate(blocks, axis=1).reshape(tile_rows, tile_cols, 3 * width)

    above = neighbour_rows(1)
    below = neighbour_rows(-1)
    qkv_grid = assemble(returned)
    extended = jnp.concatenate([above, qkv_grid[:, :, width:], below], axis=0)
    extended = extended_2(extended, (("gx", 1),), BLK)
    block_rows = tile_rows // BLK
    block_cols = tile_cols // BLK
    queries = to_blocks(qkv_grid[:, :, :width])
    key_blocks = to_blocks(extended)
    row_ids = jnp.arange(block_rows, dtype=jnp.int32)[:, None, None]
    col_ids = jnp.arange(block_cols, dtype=jnp.int32)[None, :, None]
    row_step = block_codes // 3 - 1
    col_step = block_codes % 3 - 1
    global_row = jnp.clip(
        lax.axis_index("gy") * block_rows + row_ids + row_step, 0, valid_tokens.shape[0] - 1
    )
    global_col = jnp.clip(
        lax.axis_index("gx") * block_cols + col_ids + col_step, 0, valid_tokens.shape[1] - 1
    )
    live_count = valid_tokens[global_row, global_col]
    number = block_rows * block_cols
    result = local_attention(
        queries.reshape(number, CELLS, width),
        key_blocks.reshape(-1, CELLS, 2 * width),
        block_codes.reshape(number, NBR),
        block_counts.reshape(number),
        live_count.reshape(number, NBR),
        block_cols,
    )
    return from_blocks(result.reshape(block_rows, block_cols, CELLS, width))[None]


def solution(mesh):
    return jax.shard_map(
        body,
        mesh=mesh,
        in_specs=(
            P("wa", "gy", "gx", None),
            P("wa", None),
            P("wa", None),
            P(None, ("gx", "wa")),
            P("gy", "gx", None),
            P("gy", "gx"),
            P(),
        ),
        out_specs=P("wa", "gy", "gx", None),
        check_vma=False,
    )
```

```python
import functools
import math

import jax
import jax.numpy as jnp
from jax import lax
from jax.experimental import pallas as pl
from jax.experimental.pallas import tpu as pltpu
from jax.sharding import PartitionSpec as P

D = 3072
HEADS = 12
HD = 128
BLK = 8
NBR = 9
CELLS = BLK * BLK


def extended_2(array, sides, width):
    for axis, dim in sides:
        size, length = (lax.axis_size(axis), array.shape[dim])
        up = [(i, (i + 1) % size) for i in range(size - 1)]
        down = [(j, i) for i, j in up]
        last = lax.slice_in_dim(array, length - width, length, axis=dim)
        first = lax.slice_in_dim(array, 0, width, axis=dim)
        before = lax.ppermute(last, axis, up)
        after = lax.ppermute(first, axis, down)
        array = jnp.concatenate([before, array, after], axis=dim)
    return array


def normalize(rows, shift_row, scale_row):
    widened = rows.astype(jnp.float32)
    average = jnp.mean(widened, axis=-1, keepdims=True)
    centred = widened - average
    spread = jnp.mean(centred * centred, axis=-1, keepdims=True)
    return (centred * lax.rsqrt(spread + 1e-06) * (1.0 + scale_row) + shift_row).astype(
        jnp.bfloat16
    )


def to_blocks(field):
    height, breadth, channels = field.shape
    shaped = field.reshape(height // BLK, BLK, breadth // BLK, BLK, channels)
    return shaped.transpose(0, 2, 1, 3, 4).reshape(
        height // BLK, breadth // BLK, BLK * BLK, channels
    )


def from_blocks(blocks):
    block_rows, block_cols, cells, channels = blocks.shape
    shaped = blocks.reshape(block_rows, block_cols, BLK, BLK, channels)
    return shaped.transpose(0, 2, 1, 3, 4).reshape(block_rows * BLK, block_cols * BLK, channels)


def attend_kernel(block_cols, codes_ref, counts_ref, live_ref, q_ref, kv_hbm, o_ref, kv_buf, sems):
    j = pl.program_id(0)
    n_blocks = pl.num_programs(0)
    ext_cols = block_cols + 2

    def copies(block, slot):
        out = []
        for l in range(NBR):
            code = jnp.clip(codes_ref[block * NBR + l], 0, NBR - 1)
            src = (block // block_cols + code // 3) * ext_cols + block % block_cols + code % 3
            out.append(
                pltpu.make_async_copy(
                    kv_hbm.at[src], kv_buf.at[slot, pl.ds(l * CELLS, CELLS)], sems.at[slot, l]
                )
            )
        return out

    @pl.when(j == 0)
    def _():
        for c in copies(j, 0):
            c.start()

    slot = j % 2

    @pl.when(j + 1 < n_blocks)
    def _():
        for c in copies(j + 1, 1 - slot):
            c.start()

    for c in copies(j, slot):
        c.wait()

    count = counts_ref[j]
    key_ids = lax.broadcasted_iota(jnp.int32, (CELLS, NBR * CELLS), 1)
    key_slot = key_ids // CELLS
    key_token = key_ids % CELLS
    limit = jnp.zeros((CELLS, NBR * CELLS), jnp.int32)
    for l in range(NBR):
        thr = jnp.where(l < count, live_ref[j * NBR + l], 0)
        limit = jnp.where(key_slot == l, thr, limit)
    live = key_token < limit
    width = HEADS * HD
    for h in range(HEADS):
        q = q_ref[0, :, h * HD:(h + 1) * HD]
        k = kv_buf[slot, :, h * HD:(h + 1) * HD]
        v = kv_buf[slot, :, width + h * HD:width + (h + 1) * HD]
        s = lax.dot_general(
            q, k, (((1,), (1,)), ((), ())), preferred_element_type=jnp.float32
        ) * (1.0 / math.sqrt(HD))
        s = jnp.where(live, s, -jnp.inf)
        m = jnp.max(s, axis=-1, keepdims=True)
        e = jnp.exp(s - m)
        p = (e / jnp.sum(e, axis=-1, keepdims=True)).astype(jnp.bfloat16)
        o = jnp.dot(p, v, preferred_element_type=jnp.float32)
        o_ref[0, :, h * HD:(h + 1) * HD] = o.astype(o_ref.dtype)


def local_attention(q_blocks, kv_blocks, codes, counts, live_count, block_cols):
    n_blocks = q_blocks.shape[0]
    width = q_blocks.shape[-1]
    grid_spec = pltpu.PrefetchScalarGridSpec(
        num_scalar_prefetch=3,
        grid=(n_blocks,),
        in_specs=[
            pl.BlockSpec((1, CELLS, width), lambda j, *_: (j, 0, 0)),
            pl.BlockSpec(memory_space=pl.ANY),
        ],
        out_specs=pl.BlockSpec((1, CELLS, width), lambda j, *_: (j, 0, 0)),
        scratch_shapes=[
            pltpu.VMEM((2, NBR * CELLS, 2 * width), jnp.bfloat16),
            pltpu.SemaphoreType.DMA((2, NBR)),
        ],
    )
    return pl.pallas_call(
        functools.partial(attend_kernel, block_cols),
        grid_spec=grid_spec,
        out_shape=jax.ShapeDtypeStruct(q_blocks.shape, jnp.bfloat16),
        compiler_params=pltpu.CompilerParams(dimension_semantics=("arbitrary",)),
    )(codes.reshape(-1), counts.reshape(-1), live_count.reshape(-1), q_blocks, kv_blocks)


def body(tokens, mod_shift, mod_scale, qkv_weight, block_codes, block_counts, valid_tokens):
    tile_rows = tokens.shape[1]
    tile_cols = tokens.shape[2]
    width = HEADS * HD
    group = lax.axis_size("gx")
    me = lax.axis_index("gx")
    tile = tokens[0]
    received = [tile] + [
        lax.ppermute(tile, "gx", [(i, (i + d) % group) for i in range(group)])
        for d in range(1, group)
    ]
    weight_block = lax.all_gather(qkv_weight, "wa", axis=1, tiled=True)
    strip = normalize(jnp.stack(received), mod_shift[0], mod_scale[0]).reshape(
        group, tile_rows * tile_cols, D
    )
    partial = [
        jnp.dot(strip[d], weight_block, preferred_element_type=jnp.float32).astype(jnp.bfloat16)
        for d in range(group)
    ]
    partial[0] = lax.optimization_barrier(partial[0])
    returned = [partial[0]] + [
        lax.ppermute(partial[d], "gx", [(i, (i - d) % group) for i in range(group)])
        for d in range(1, group)
    ]
    rows_axis = lax.axis_size("gy")
    block = partial[0].shape[-1]
    senders = [g for g in range(group) if (g + 1) * block > width]

    def neighbour_rows(step):
        chunks = []
        for d in range(group):
            pairs = [
                (r * group + g, (r + step) * group + (g - d) % group)
                for r in range(rows_axis)
                if 0 <= r + step < rows_axis
                for g in senders
            ]
            chunks.append(lax.ppermute(partial[d], ("gy", "gx"), pairs))
        return assemble(chunks)[:, :, width:]

    def assemble(chunks):
        blocks = []
        for b in range(group):
            pick = (b - me) % group
            chosen = chunks[0]
            for d in range(1, group):
                chosen = jnp.where(pick == d, chunks[d], chosen)
            blocks.append(chosen)
        return jnp.concatenate(blocks, axis=1).reshape(tile_rows, tile_cols, 3 * width)

    above = neighbour_rows(1)
    below = neighbour_rows(-1)
    qkv_grid = assemble(returned)
    extended = jnp.concatenate([above, qkv_grid[:, :, width:], below], axis=0)
    extended = extended_2(extended, (("gx", 1),), BLK)
    block_rows = tile_rows // BLK
    block_cols = tile_cols // BLK
    queries = to_blocks(qkv_grid[:, :, :width])
    key_blocks = to_blocks(extended)
    row_ids = jnp.arange(block_rows, dtype=jnp.int32)[:, None, None]
    col_ids = jnp.arange(block_cols, dtype=jnp.int32)[None, :, None]
    row_step = block_codes // 3 - 1
    col_step = block_codes % 3 - 1
    global_row = jnp.clip(
        lax.axis_index("gy") * block_rows + row_ids + row_step, 0, valid_tokens.shape[0] - 1
    )
    global_col = jnp.clip(
        lax.axis_index("gx") * block_cols + col_ids + col_step, 0, valid_tokens.shape[1] - 1
    )
    live_count = valid_tokens[global_row, global_col]
    number = block_rows * block_cols
    result = local_attention(
        queries.reshape(number, CELLS, width),
        key_blocks.reshape(-1, CELLS, 2 * width),
        block_codes.reshape(number, NBR),
        block_counts.reshape(number),
        live_count.reshape(number, NBR),
        block_cols,
    )
    return from_blocks(result.reshape(block_rows, block_cols, CELLS, width))[None]


def solution(mesh):
    return jax.shard_map(
        body,
        mesh=mesh,
        in_specs=(
            P("wa", "gy", "gx", None),
            P("wa", None),
            P("wa", None),
            P(None, ("gx", "wa")),
            P("gy", "gx", None),
            P("gy", "gx"),
            P(),
        ),
        out_specs=P("wa", "gy", "gx", None),
        check_vma=False,
    )
```

```python
import functools
import math

import jax
import jax.numpy as jnp
from jax import lax
from jax.experimental import pallas as pl
from jax.experimental.pallas import tpu as pltpu
from jax.sharding import PartitionSpec as P

D = 3072
HEADS = 12
HD = 128
BLK = 8
NBR = 9
CELLS = BLK * BLK


def extended_2(array, sides, width):
    for axis, dim in sides:
        size, length = (lax.axis_size(axis), array.shape[dim])
        up = [(i, (i + 1) % size) for i in range(size - 1)]
        down = [(j, i) for i, j in up]
        last = lax.slice_in_dim(array, length - width, length, axis=dim)
        first = lax.slice_in_dim(array, 0, width, axis=dim)
        before = lax.ppermute(last, axis, up)
        after = lax.ppermute(first, axis, down)
        array = jnp.concatenate([before, array, after], axis=dim)
    return array


def normalize(rows, shift_row, scale_row):
    widened = rows.astype(jnp.float32)
    average = jnp.mean(widened, axis=-1, keepdims=True)
    centred = widened - average
    spread = jnp.mean(centred * centred, axis=-1, keepdims=True)
    return (centred * lax.rsqrt(spread + 1e-06) * (1.0 + scale_row) + shift_row).astype(
        jnp.bfloat16
    )


def to_blocks(field):
    height, breadth, channels = field.shape
    shaped = field.reshape(height // BLK, BLK, breadth // BLK, BLK, channels)
    return shaped.transpose(0, 2, 1, 3, 4).reshape(
        height // BLK, breadth // BLK, BLK * BLK, channels
    )


def from_blocks(blocks):
    block_rows, block_cols, cells, channels = blocks.shape
    shaped = blocks.reshape(block_rows, block_cols, BLK, BLK, channels)
    return shaped.transpose(0, 2, 1, 3, 4).reshape(block_rows * BLK, block_cols * BLK, channels)


def attend_kernel(block_cols, codes_ref, counts_ref, live_ref, q_ref, kv_hbm, o_ref, kv_buf, sems):
    j = pl.program_id(0)
    n_blocks = pl.num_programs(0)
    ext_cols = block_cols + 2

    def copies(block, slot):
        out = []
        for l in range(NBR):
            code = jnp.clip(codes_ref[block * NBR + l], 0, NBR - 1)
            src = (block // block_cols + code // 3) * ext_cols + block % block_cols + code % 3
            out.append(
                pltpu.make_async_copy(
                    kv_hbm.at[src], kv_buf.at[slot, pl.ds(l * CELLS, CELLS)], sems.at[slot, l]
                )
            )
        return out

    @pl.when(j == 0)
    def _():
        for c in copies(j, 0):
            c.start()

    slot = j % 2

    @pl.when(j + 1 < n_blocks)
    def _():
        for c in copies(j + 1, 1 - slot):
            c.start()

    for c in copies(j, slot):
        c.wait()

    count = counts_ref[j]
    key_ids = lax.broadcasted_iota(jnp.int32, (CELLS, NBR * CELLS), 1)
    key_slot = key_ids // CELLS
    key_token = key_ids % CELLS
    limit = jnp.zeros((CELLS, NBR * CELLS), jnp.int32)
    for l in range(NBR):
        thr = jnp.where(l < count, live_ref[j * NBR + l], 0)
        limit = jnp.where(key_slot == l, thr, limit)
    live = key_token < limit
    width = HEADS * HD
    for h in range(HEADS):
        q = q_ref[:, :, h * HD:(h + 1) * HD].astype(jnp.float32).reshape(CELLS, HD)
        q = q.astype(jnp.bfloat16)
        k = kv_buf[slot, :, h * HD:(h + 1) * HD]
        v = kv_buf[slot, :, width + h * HD:width + (h + 1) * HD]
        s = lax.dot_general(
            q, k, (((1,), (1,)), ((), ())), preferred_element_type=jnp.float32
        ) * (1.0 / math.sqrt(HD))
        s = jnp.where(live, s, -jnp.inf)
        m = jnp.max(s, axis=-1, keepdims=True)
        e = jnp.exp(s - m)
        p = (e / jnp.sum(e, axis=-1, keepdims=True)).astype(jnp.bfloat16)
        o = jnp.dot(p, v, preferred_element_type=jnp.float32)
        o_ref[:, :, h * HD:(h + 1) * HD] = o.reshape(BLK, BLK, HD).astype(o_ref.dtype)


def local_attention(q_grid, kv_blocks, codes, counts, live_count, block_cols):
    rows = q_grid.shape[0]
    width = HEADS * HD
    grid_spec = pltpu.PrefetchScalarGridSpec(
        num_scalar_prefetch=3,
        grid=(block_cols,),
        in_specs=[
            pl.BlockSpec((rows, BLK, width), lambda j, *_: (0, j, 0)),
            pl.BlockSpec(memory_space=pl.ANY),
        ],
        out_specs=pl.BlockSpec((rows, BLK, width), lambda j, *_: (0, j, 0)),
        scratch_shapes=[
            pltpu.VMEM((2, NBR * CELLS, 2 * width), jnp.bfloat16),
            pltpu.SemaphoreType.DMA((2, NBR)),
        ],
    )
    return pl.pallas_call(
        functools.partial(attend_kernel, block_cols),
        grid_spec=grid_spec,
        out_shape=jax.ShapeDtypeStruct((rows, q_grid.shape[1], width), jnp.bfloat16),
        compiler_params=pltpu.CompilerParams(dimension_semantics=("arbitrary",)),
    )(codes.reshape(-1), counts.reshape(-1), live_count.reshape(-1), q_grid, kv_blocks)


def body(tokens, mod_shift, mod_scale, qkv_weight, block_codes, block_counts, valid_tokens):
    tile_rows = tokens.shape[1]
    tile_cols = tokens.shape[2]
    width = HEADS * HD
    group = lax.axis_size("gx")
    me = lax.axis_index("gx")
    tile = tokens[0]
    received = [tile] + [
        lax.ppermute(tile, "gx", [(i, (i + d) % group) for i in range(group)])
        for d in range(1, group)
    ]
    weight_block = lax.all_gather(qkv_weight, "wa", axis=1, tiled=True)
    strip = normalize(jnp.stack(received), mod_shift[0], mod_scale[0]).reshape(
        group, tile_rows * tile_cols, D
    )
    partial = [
        jnp.dot(strip[d], weight_block, preferred_element_type=jnp.float32).astype(jnp.bfloat16)
        for d in range(group)
    ]
    partial[0] = lax.optimization_barrier(partial[0])
    returned = [partial[0]] + [
        lax.ppermute(partial[d], "gx", [(i, (i - d) % group) for i in range(group)])
        for d in range(1, group)
    ]
    rows_axis = lax.axis_size("gy")
    block = partial[0].shape[-1]
    senders = [g for g in range(group) if (g + 1) * block > width]

    def neighbour_rows(step):
        chunks = []
        for d in range(group):
            pairs = [
                (r * group + g, (r + step) * group + (g - d) % group)
                for r in range(rows_axis)
                if 0 <= r + step < rows_axis
                for g in senders
            ]
            chunks.append(lax.ppermute(partial[d], ("gy", "gx"), pairs))
        return assemble(chunks)[:, :, width:]

    def assemble(chunks):
        blocks = []
        for b in range(group):
            pick = (b - me) % group
            chosen = chunks[0]
            for d in range(1, group):
                chosen = jnp.where(pick == d, chunks[d], chosen)
            blocks.append(chosen)
        return jnp.concatenate(blocks, axis=1).reshape(tile_rows, tile_cols, 3 * width)

    above = neighbour_rows(1)
    below = neighbour_rows(-1)
    qkv_grid = assemble(returned)
    extended = jnp.concatenate([above, qkv_grid[:, :, width:], below], axis=0)
    extended = extended_2(extended, (("gx", 1),), BLK)
    block_rows = tile_rows // BLK
    block_cols = tile_cols // BLK
    queries = to_blocks(qkv_grid[:, :, :width])
    key_blocks = to_blocks(extended)
    row_ids = jnp.arange(block_rows, dtype=jnp.int32)[:, None, None]
    col_ids = jnp.arange(block_cols, dtype=jnp.int32)[None, :, None]
    row_step = block_codes // 3 - 1
    col_step = block_codes % 3 - 1
    global_row = jnp.clip(
        lax.axis_index("gy") * block_rows + row_ids + row_step, 0, valid_tokens.shape[0] - 1
    )
    global_col = jnp.clip(
        lax.axis_index("gx") * block_cols + col_ids + col_step, 0, valid_tokens.shape[1] - 1
    )
    live_count = valid_tokens[global_row, global_col]
    number = block_rows * block_cols
    result = local_attention(
        qkv_grid,
        key_blocks.reshape(-1, CELLS, 2 * width),
        block_codes.reshape(number, NBR),
        block_counts.reshape(number),
        live_count.reshape(number, NBR),
        block_cols,
    )
    return result[None]


def solution(mesh):
    return jax.shard_map(
        body,
        mesh=mesh,
        in_specs=(
            P("wa", "gy", "gx", None),
            P("wa", None),
            P("wa", None),
            P(None, ("gx", "wa")),
            P("gy", "gx", None),
            P("gy", "gx"),
            P(),
        ),
        out_specs=P("wa", "gy", "gx", None),
        check_vma=False,
    )
```

```python
import functools
import math

import jax
import jax.numpy as jnp
from jax import lax
from jax.experimental import pallas as pl
from jax.experimental.pallas import tpu as pltpu
from jax.sharding import PartitionSpec as P

D = 3072
HEADS = 12
HD = 128
BLK = 8
NBR = 9
CELLS = BLK * BLK


def extended_2(array, sides, width):
    for axis, dim in sides:
        size, length = (lax.axis_size(axis), array.shape[dim])
        up = [(i, (i + 1) % size) for i in range(size - 1)]
        down = [(j, i) for i, j in up]
        last = lax.slice_in_dim(array, length - width, length, axis=dim)
        first = lax.slice_in_dim(array, 0, width, axis=dim)
        before = lax.ppermute(last, axis, up)
        after = lax.ppermute(first, axis, down)
        array = jnp.concatenate([before, array, after], axis=dim)
    return array


def normalize(rows, shift_row, scale_row):
    widened = rows.astype(jnp.float32)
    average = jnp.mean(widened, axis=-1, keepdims=True)
    centred = widened - average
    spread = jnp.mean(centred * centred, axis=-1, keepdims=True)
    return (centred * lax.rsqrt(spread + 1e-06) * (1.0 + scale_row) + shift_row).astype(
        jnp.bfloat16
    )


def to_blocks(field):
    height, breadth, channels = field.shape
    shaped = field.reshape(height // BLK, BLK, breadth // BLK, BLK, channels)
    return shaped.transpose(0, 2, 1, 3, 4).reshape(
        height // BLK, breadth // BLK, BLK * BLK, channels
    )


def from_blocks(blocks):
    block_rows, block_cols, cells, channels = blocks.shape
    shaped = blocks.reshape(block_rows, block_cols, BLK, BLK, channels)
    return shaped.transpose(0, 2, 1, 3, 4).reshape(block_rows * BLK, block_cols * BLK, channels)


def attend_kernel(
    block_cols, codes_ref, counts_ref, live_ref, q_ref, kv_mid, kv_left, kv_right, o_ref, kv_buf, sems
):
    j = pl.program_id(0)
    n_blocks = pl.num_programs(0)

    def start(block, slot):
        for l in range(NBR):
            code = jnp.clip(codes_ref[block * NBR + l], 0, NBR - 1)
            row = block // block_cols + code // 3
            col = block % block_cols + code % 3 - 1
            dst = kv_buf.at[slot, pl.ds(l * CELLS, CELLS)]
            mid = row * block_cols + jnp.clip(col, 0, block_cols - 1)

            @pl.when(col < 0)
            def _():
                pltpu.make_async_copy(kv_left.at[row], dst, sems.at[slot, l]).start()

            @pl.when(col >= block_cols)
            def _():
                pltpu.make_async_copy(kv_right.at[row], dst, sems.at[slot, l]).start()

            @pl.when((col >= 0) & (col < block_cols))
            def _():
                pltpu.make_async_copy(kv_mid.at[mid], dst, sems.at[slot, l]).start()

    @pl.when(j == 0)
    def _():
        start(j, 0)

    slot = j % 2

    @pl.when(j + 1 < n_blocks)
    def _():
        start(j + 1, 1 - slot)

    for l in range(NBR):
        pltpu.make_async_copy(
            kv_mid.at[0], kv_buf.at[slot, pl.ds(l * CELLS, CELLS)], sems.at[slot, l]
        ).wait()

    count = counts_ref[j]
    key_ids = lax.broadcasted_iota(jnp.int32, (CELLS, NBR * CELLS), 1)
    key_slot = key_ids // CELLS
    key_token = key_ids % CELLS
    limit = jnp.zeros((CELLS, NBR * CELLS), jnp.int32)
    for l in range(NBR):
        thr = jnp.where(l < count, live_ref[j * NBR + l], 0)
        limit = jnp.where(key_slot == l, thr, limit)
    live = key_token < limit
    width = HEADS * HD
    for h in range(HEADS):
        q = q_ref[:, :, h * HD:(h + 1) * HD].astype(jnp.float32).reshape(CELLS, HD)
        q = q.astype(jnp.bfloat16)
        k = kv_buf[slot, :, h * HD:(h + 1) * HD]
        v = kv_buf[slot, :, width + h * HD:width + (h + 1) * HD]
        s = lax.dot_general(
            q, k, (((1,), (1,)), ((), ())), preferred_element_type=jnp.float32
        ) * (1.0 / math.sqrt(HD))
        s = jnp.where(live, s, -jnp.inf)
        m = jnp.max(s, axis=-1, keepdims=True)
        e = jnp.exp(s - m)
        p = (e / jnp.sum(e, axis=-1, keepdims=True)).astype(jnp.bfloat16)
        o = jnp.dot(p, v, preferred_element_type=jnp.float32)
        o_ref[:, :, h * HD:(h + 1) * HD] = o.reshape(BLK, BLK, HD).astype(o_ref.dtype)


def local_attention(q_grid, kv_mid, kv_left, kv_right, codes, counts, live_count, block_cols):
    rows = q_grid.shape[0]
    width = HEADS * HD
    grid_spec = pltpu.PrefetchScalarGridSpec(
        num_scalar_prefetch=3,
        grid=(block_cols,),
        in_specs=[
            pl.BlockSpec((rows, BLK, width), lambda j, *_: (0, j, 0)),
            pl.BlockSpec(memory_space=pl.ANY),
            pl.BlockSpec(memory_space=pl.ANY),
            pl.BlockSpec(memory_space=pl.ANY),
        ],
        out_specs=pl.BlockSpec((rows, BLK, width), lambda j, *_: (0, j, 0)),
        scratch_shapes=[
            pltpu.VMEM((2, NBR * CELLS, 2 * width), jnp.bfloat16),
            pltpu.SemaphoreType.DMA((2, NBR)),
        ],
    )
    return pl.pallas_call(
        functools.partial(attend_kernel, block_cols),
        grid_spec=grid_spec,
        out_shape=jax.ShapeDtypeStruct((rows, q_grid.shape[1], width), jnp.bfloat16),
        compiler_params=pltpu.CompilerParams(dimension_semantics=("arbitrary",)),
    )(codes.reshape(-1), counts.reshape(-1), live_count.reshape(-1), q_grid, kv_mid, kv_left, kv_right)


def body(tokens, mod_shift, mod_scale, qkv_weight, block_codes, block_counts, valid_tokens):
    tile_rows = tokens.shape[1]
    tile_cols = tokens.shape[2]
    width = HEADS * HD
    group = lax.axis_size("gx")
    me = lax.axis_index("gx")
    tile = tokens[0]
    received = [tile] + [
        lax.ppermute(tile, "gx", [(i, (i + d) % group) for i in range(group)])
        for d in range(1, group)
    ]
    weight_block = lax.all_gather(qkv_weight, "wa", axis=1, tiled=True)
    strip = normalize(jnp.stack(received), mod_shift[0], mod_scale[0]).reshape(
        group, tile_rows * tile_cols, D
    )
    partial = [
        jnp.dot(strip[d], weight_block, preferred_element_type=jnp.float32).astype(jnp.bfloat16)
        for d in range(group)
    ]
    partial[0] = lax.optimization_barrier(partial[0])
    returned = [partial[0]] + [
        lax.ppermute(partial[d], "gx", [(i, (i - d) % group) for i in range(group)])
        for d in range(1, group)
    ]
    rows_axis = lax.axis_size("gy")
    block = partial[0].shape[-1]
    senders = [g for g in range(group) if (g + 1) * block > width]

    def neighbour_rows(step):
        chunks = []
        for d in range(group):
            pairs = [
                (r * group + g, (r + step) * group + (g - d) % group)
                for r in range(rows_axis)
                if 0 <= r + step < rows_axis
                for g in senders
            ]
            chunks.append(lax.ppermute(partial[d], ("gy", "gx"), pairs))
        return assemble(chunks)[:, :, width:]

    def assemble(chunks):
        blocks = []
        for b in range(group):
            pick = (b - me) % group
            chosen = chunks[0]
            for d in range(1, group):
                chosen = jnp.where(pick == d, chunks[d], chosen)
            blocks.append(chosen)
        return jnp.concatenate(blocks, axis=1).reshape(tile_rows, tile_cols, 3 * width)

    above = neighbour_rows(1)
    below = neighbour_rows(-1)
    qkv_grid = assemble(returned)
    middle = to_blocks(jnp.concatenate([above, qkv_grid[:, :, width:], below], axis=0))
    col_up = [(i, i + 1) for i in range(group - 1)]
    col_down = [(i + 1, i) for i in range(group - 1)]
    left = lax.ppermute(middle[:, -1], "gx", col_up)
    right = lax.ppermute(middle[:, 0], "gx", col_down)
    block_rows = tile_rows // BLK
    block_cols = tile_cols // BLK
    queries = to_blocks(qkv_grid[:, :, :width])
    row_ids = jnp.arange(block_rows, dtype=jnp.int32)[:, None, None]
    col_ids = jnp.arange(block_cols, dtype=jnp.int32)[None, :, None]
    row_step = block_codes // 3 - 1
    col_step = block_codes % 3 - 1
    global_row = jnp.clip(
        lax.axis_index("gy") * block_rows + row_ids + row_step, 0, valid_tokens.shape[0] - 1
    )
    global_col = jnp.clip(
        lax.axis_index("gx") * block_cols + col_ids + col_step, 0, valid_tokens.shape[1] - 1
    )
    live_count = valid_tokens[global_row, global_col]
    number = block_rows * block_cols
    result = local_attention(
        qkv_grid,
        middle.reshape(-1, CELLS, 2 * width),
        left,
        right,
        block_codes.reshape(number, NBR),
        block_counts.reshape(number),
        live_count.reshape(number, NBR),
        block_cols,
    )
    return result[None]


def solution(mesh):
    return jax.shard_map(
        body,
        mesh=mesh,
        in_specs=(
            P("wa", "gy", "gx", None),
            P("wa", None),
            P("wa", None),
            P(None, ("gx", "wa")),
            P("gy", "gx", None),
            P("gy", "gx"),
            P(),
        ),
        out_specs=P("wa", "gy", "gx", None),
        check_vma=False,
    )
```

```python
import functools
import math

import jax
import jax.numpy as jnp
from jax import lax
from jax.experimental import pallas as pl
from jax.experimental.pallas import tpu as pltpu
from jax.sharding import PartitionSpec as P

D = 3072
HEADS = 12
HD = 128
BLK = 8
NBR = 9
CELLS = BLK * BLK


def extended_2(array, sides, width):
    for axis, dim in sides:
        size, length = (lax.axis_size(axis), array.shape[dim])
        up = [(i, (i + 1) % size) for i in range(size - 1)]
        down = [(j, i) for i, j in up]
        last = lax.slice_in_dim(array, length - width, length, axis=dim)
        first = lax.slice_in_dim(array, 0, width, axis=dim)
        before = lax.ppermute(last, axis, up)
        after = lax.ppermute(first, axis, down)
        array = jnp.concatenate([before, array, after], axis=dim)
    return array


def normalize(rows, shift_row, scale_row):
    widened = rows.astype(jnp.float32)
    average = jnp.mean(widened, axis=-1, keepdims=True)
    centred = widened - average
    spread = jnp.mean(centred * centred, axis=-1, keepdims=True)
    return (centred * lax.rsqrt(spread + 1e-06) * (1.0 + scale_row) + shift_row).astype(
        jnp.bfloat16
    )


def to_blocks(field):
    height, breadth, channels = field.shape
    shaped = field.reshape(height // BLK, BLK, breadth // BLK, BLK, channels)
    return shaped.transpose(0, 2, 1, 3, 4).reshape(
        height // BLK, breadth // BLK, BLK * BLK, channels
    )


def from_blocks(blocks):
    block_rows, block_cols, cells, channels = blocks.shape
    shaped = blocks.reshape(block_rows, block_cols, BLK, BLK, channels)
    return shaped.transpose(0, 2, 1, 3, 4).reshape(block_rows * BLK, block_cols * BLK, channels)


def attend_kernel(block_cols, base, stride, sides, codes_ref, counts_ref, live_ref, q_ref, kv_mid, *rest):
    if sides:
        kv_left, kv_right, _, o_ref, kv_buf, sems = rest
    else:
        o_ref, kv_buf, sems = rest
    step = pl.program_id(0)
    n_steps = pl.num_programs(0)

    def start(at, slot):
        block = base + at * stride
        for l in range(NBR):
            code = jnp.clip(codes_ref[block * NBR + l], 0, NBR - 1)
            row = block // block_cols + code // 3
            col = block % block_cols + code % 3 - 1
            dst = kv_buf.at[slot, pl.ds(l * CELLS, CELLS)]
            mid = row * block_cols + jnp.clip(col, 0, block_cols - 1)

            if not sides:
                pltpu.make_async_copy(kv_mid.at[mid], dst, sems.at[slot, l]).start()
                continue

            @pl.when(col < 0)
            def _():
                pltpu.make_async_copy(kv_left.at[row], dst, sems.at[slot, l]).start()

            @pl.when(col >= block_cols)
            def _():
                pltpu.make_async_copy(kv_right.at[row], dst, sems.at[slot, l]).start()

            @pl.when((col >= 0) & (col < block_cols))
            def _():
                pltpu.make_async_copy(kv_mid.at[mid], dst, sems.at[slot, l]).start()

    @pl.when(step == 0)
    def _():
        start(step, 0)

    slot = step % 2

    @pl.when(step + 1 < n_steps)
    def _():
        start(step + 1, 1 - slot)

    j = base + step * stride

    for l in range(NBR):
        pltpu.make_async_copy(
            kv_mid.at[0], kv_buf.at[slot, pl.ds(l * CELLS, CELLS)], sems.at[slot, l]
        ).wait()

    count = counts_ref[j]
    key_ids = lax.broadcasted_iota(jnp.int32, (CELLS, NBR * CELLS), 1)
    key_slot = key_ids // CELLS
    key_token = key_ids % CELLS
    limit = jnp.zeros((CELLS, NBR * CELLS), jnp.int32)
    for l in range(NBR):
        thr = jnp.where(l < count, live_ref[j * NBR + l], 0)
        limit = jnp.where(key_slot == l, thr, limit)
    live = key_token < limit
    width = HEADS * HD
    for h in range(HEADS):
        q = q_ref[:, :, h * HD:(h + 1) * HD].astype(jnp.float32).reshape(CELLS, HD)
        q = q.astype(jnp.bfloat16)
        k = kv_buf[slot, :, h * HD:(h + 1) * HD]
        v = kv_buf[slot, :, width + h * HD:width + (h + 1) * HD]
        s = lax.dot_general(
            q, k, (((1,), (1,)), ((), ())), preferred_element_type=jnp.float32
        ) * (1.0 / math.sqrt(HD))
        s = jnp.where(live, s, -jnp.inf)
        m = jnp.max(s, axis=-1, keepdims=True)
        e = jnp.exp(s - m)
        p = (e / jnp.sum(e, axis=-1, keepdims=True)).astype(jnp.bfloat16)
        o = jnp.dot(p, v, preferred_element_type=jnp.float32)
        o_ref[:, :, h * HD:(h + 1) * HD] = o.reshape(BLK, BLK, HD).astype(o_ref.dtype)


def attention_call(q_grid, kv_mid, sides, codes, counts, live_count, block_cols, base, stride, steps):
    rows = q_grid.shape[0]
    width = HEADS * HD
    in_specs = [
        pl.BlockSpec((rows, BLK, width), lambda i, *_: (0, base + i * stride, 0)),
        pl.BlockSpec(memory_space=pl.ANY),
    ]
    operands = [q_grid, kv_mid]
    aliases = {}
    if sides is not None:
        in_specs += [pl.BlockSpec(memory_space=pl.ANY)] * 3
        operands += list(sides)
        aliases = {3 + len(operands) - 1: 0}
    grid_spec = pltpu.PrefetchScalarGridSpec(
        num_scalar_prefetch=3,
        grid=(steps,),
        in_specs=in_specs,
        out_specs=pl.BlockSpec((rows, BLK, width), lambda i, *_: (0, base + i * stride, 0)),
        scratch_shapes=[
            pltpu.VMEM((2, NBR * CELLS, 2 * width), jnp.bfloat16),
            pltpu.SemaphoreType.DMA((2, NBR)),
        ],
    )
    return pl.pallas_call(
        functools.partial(attend_kernel, block_cols, base, stride, sides is not None),
        grid_spec=grid_spec,
        out_shape=jax.ShapeDtypeStruct((rows, q_grid.shape[1], width), jnp.bfloat16),
        input_output_aliases=aliases,
        compiler_params=pltpu.CompilerParams(dimension_semantics=("arbitrary",)),
    )(codes.reshape(-1), counts.reshape(-1), live_count.reshape(-1), *operands)


def local_attention(q_grid, kv_mid, kv_left, kv_right, codes, counts, live_count, block_cols):
    inner = attention_call(
        q_grid, kv_mid, None, codes, counts, live_count, block_cols, 1, 1, block_cols - 2
    )
    return attention_call(
        q_grid, kv_mid, (kv_left, kv_right, inner), codes, counts, live_count,
        block_cols, 0, block_cols - 1, 2,
    )


def body(tokens, mod_shift, mod_scale, qkv_weight, block_codes, block_counts, valid_tokens):
    tile_rows = tokens.shape[1]
    tile_cols = tokens.shape[2]
    width = HEADS * HD
    group = lax.axis_size("gx")
    me = lax.axis_index("gx")
    tile = tokens[0]
    received = [tile] + [
        lax.ppermute(tile, "gx", [(i, (i + d) % group) for i in range(group)])
        for d in range(1, group)
    ]
    weight_block = lax.all_gather(qkv_weight, "wa", axis=1, tiled=True)
    strip = normalize(jnp.stack(received), mod_shift[0], mod_scale[0]).reshape(
        group, tile_rows * tile_cols, D
    )
    partial = [
        jnp.dot(strip[d], weight_block, preferred_element_type=jnp.float32).astype(jnp.bfloat16)
        for d in range(group)
    ]
    partial[0] = lax.optimization_barrier(partial[0])
    returned = [partial[0]] + [
        lax.ppermute(partial[d], "gx", [(i, (i - d) % group) for i in range(group)])
        for d in range(1, group)
    ]
    rows_axis = lax.axis_size("gy")
    block = partial[0].shape[-1]
    senders = [g for g in range(group) if (g + 1) * block > width]

    def neighbour_rows(step):
        chunks = []
        for d in range(group):
            pairs = [
                (r * group + g, (r + step) * group + (g - d) % group)
                for r in range(rows_axis)
                if 0 <= r + step < rows_axis
                for g in senders
            ]
            chunks.append(lax.ppermute(partial[d], ("gy", "gx"), pairs))
        return assemble(chunks)[:, :, width:]

    def assemble(chunks):
        blocks = []
        for b in range(group):
            pick = (b - me) % group
            chosen = chunks[0]
            for d in range(1, group):
                chosen = jnp.where(pick == d, chunks[d], chosen)
            blocks.append(chosen)
        return jnp.concatenate(blocks, axis=1).reshape(tile_rows, tile_cols, 3 * width)

    above = neighbour_rows(1)
    below = neighbour_rows(-1)
    qkv_grid = assemble(returned)
    middle = to_blocks(jnp.concatenate([above, qkv_grid[:, :, width:], below], axis=0))
    col_up = [(i, i + 1) for i in range(group - 1)]
    col_down = [(i + 1, i) for i in range(group - 1)]
    left = lax.ppermute(middle[:, -1], "gx", col_up)
    right = lax.ppermute(middle[:, 0], "gx", col_down)
    block_rows = tile_rows // BLK
    block_cols = tile_cols // BLK
    queries = to_blocks(qkv_grid[:, :, :width])
    row_ids = jnp.arange(block_rows, dtype=jnp.int32)[:, None, None]
    col_ids = jnp.arange(block_cols, dtype=jnp.int32)[None, :, None]
    row_step = block_codes // 3 - 1
    col_step = block_codes % 3 - 1
    global_row = jnp.clip(
        lax.axis_index("gy") * block_rows + row_ids + row_step, 0, valid_tokens.shape[0] - 1
    )
    global_col = jnp.clip(
        lax.axis_index("gx") * block_cols + col_ids + col_step, 0, valid_tokens.shape[1] - 1
    )
    live_count = valid_tokens[global_row, global_col]
    number = block_rows * block_cols
    result = local_attention(
        qkv_grid,
        middle.reshape(-1, CELLS, 2 * width),
        left,
        right,
        block_codes.reshape(number, NBR),
        block_counts.reshape(number),
        live_count.reshape(number, NBR),
        block_cols,
    )
    return result[None]


def solution(mesh):
    return jax.shard_map(
        body,
        mesh=mesh,
        in_specs=(
            P("wa", "gy", "gx", None),
            P("wa", None),
            P("wa", None),
            P(None, ("gx", "wa")),
            P("gy", "gx", None),
            P("gy", "gx"),
            P(),
        ),
        out_specs=P("wa", "gy", "gx", None),
        check_vma=False,
    )
```

```python
import functools
import math

import jax
import jax.numpy as jnp
from jax import lax
from jax.experimental import pallas as pl
from jax.experimental.pallas import tpu as pltpu
from jax.sharding import PartitionSpec as P

D = 3072
HEADS = 12
HD = 128
BLK = 8
NBR = 9
CELLS = BLK * BLK


def extended_2(array, sides, width):
    for axis, dim in sides:
        size, length = (lax.axis_size(axis), array.shape[dim])
        up = [(i, (i + 1) % size) for i in range(size - 1)]
        down = [(j, i) for i, j in up]
        last = lax.slice_in_dim(array, length - width, length, axis=dim)
        first = lax.slice_in_dim(array, 0, width, axis=dim)
        before = lax.ppermute(last, axis, up)
        after = lax.ppermute(first, axis, down)
        array = jnp.concatenate([before, array, after], axis=dim)
    return array


def normalize(rows, shift_row, scale_row):
    widened = rows.astype(jnp.float32)
    average = jnp.mean(widened, axis=-1, keepdims=True)
    centred = widened - average
    spread = jnp.mean(centred * centred, axis=-1, keepdims=True)
    return (centred * lax.rsqrt(spread + 1e-06) * (1.0 + scale_row) + shift_row).astype(
        jnp.bfloat16
    )


def to_blocks(field):
    height, breadth, channels = field.shape
    shaped = field.reshape(height // BLK, BLK, breadth // BLK, BLK, channels)
    return shaped.transpose(0, 2, 1, 3, 4).reshape(
        height // BLK, breadth // BLK, BLK * BLK, channels
    )


def from_blocks(blocks):
    block_rows, block_cols, cells, channels = blocks.shape
    shaped = blocks.reshape(block_rows, block_cols, BLK, BLK, channels)
    return shaped.transpose(0, 2, 1, 3, 4).reshape(block_rows * BLK, block_cols * BLK, channels)


def attend_kernel(
    block_cols, codes_ref, counts_ref, live_ref, q_ref, kv_mid, kv_left, kv_right, o_ref, kv_buf, sems
):
    j = pl.program_id(0)
    n_blocks = pl.num_programs(0)

    def start(block, slot):
        for l in range(NBR):
            code = jnp.clip(codes_ref[block * NBR + l], 0, NBR - 1)
            row = block // block_cols + code // 3
            col = block % block_cols + code % 3 - 1
            dst = kv_buf.at[slot, pl.ds(l * CELLS, CELLS)]
            mid = row * block_cols + jnp.clip(col, 0, block_cols - 1)

            @pl.when(col < 0)
            def _():
                pltpu.make_async_copy(kv_left.at[row], dst, sems.at[slot, l]).start()

            @pl.when(col >= block_cols)
            def _():
                pltpu.make_async_copy(kv_right.at[row], dst, sems.at[slot, l]).start()

            @pl.when((col >= 0) & (col < block_cols))
            def _():
                pltpu.make_async_copy(kv_mid.at[mid], dst, sems.at[slot, l]).start()

    @pl.when(j == 0)
    def _():
        start(j, 0)

    slot = j % 2

    @pl.when(j + 1 < n_blocks)
    def _():
        start(j + 1, 1 - slot)

    for l in range(NBR):
        pltpu.make_async_copy(
            kv_mid.at[0], kv_buf.at[slot, pl.ds(l * CELLS, CELLS)], sems.at[slot, l]
        ).wait()

    count = counts_ref[j]
    key_ids = lax.broadcasted_iota(jnp.int32, (CELLS, NBR * CELLS), 1)
    key_slot = key_ids // CELLS
    key_token = key_ids % CELLS
    limit = jnp.zeros((CELLS, NBR * CELLS), jnp.int32)
    for l in range(NBR):
        thr = jnp.where(l < count, live_ref[j * NBR + l], 0)
        limit = jnp.where(key_slot == l, thr, limit)
    bias = jnp.where(key_token < limit, 0.0, -jnp.inf).astype(jnp.float32)
    width = HEADS * HD
    for h in range(HEADS):
        q = q_ref[:, :, h * HD:(h + 1) * HD].astype(jnp.float32).reshape(CELLS, HD)
        q = q.astype(jnp.bfloat16)
        k = kv_buf[slot, :, h * HD:(h + 1) * HD]
        v = kv_buf[slot, :, width + h * HD:width + (h + 1) * HD]
        s = lax.dot_general(
            q, k, (((1,), (1,)), ((), ())), preferred_element_type=jnp.float32
        ) * (1.0 / math.sqrt(HD))
        s = s + bias
        m = jnp.max(s, axis=-1, keepdims=True)
        e = jnp.exp(s - m)
        p = (e * (1.0 / jnp.sum(e, axis=-1, keepdims=True))).astype(jnp.bfloat16)
        o = jnp.dot(p, v, preferred_element_type=jnp.float32)
        o_ref[:, :, h * HD:(h + 1) * HD] = o.reshape(BLK, BLK, HD).astype(o_ref.dtype)


def local_attention(q_grid, kv_mid, kv_left, kv_right, codes, counts, live_count, block_cols):
    rows = q_grid.shape[0]
    width = HEADS * HD
    grid_spec = pltpu.PrefetchScalarGridSpec(
        num_scalar_prefetch=3,
        grid=(block_cols,),
        in_specs=[
            pl.BlockSpec((rows, BLK, width), lambda j, *_: (0, j, 0)),
            pl.BlockSpec(memory_space=pl.ANY),
            pl.BlockSpec(memory_space=pl.ANY),
            pl.BlockSpec(memory_space=pl.ANY),
        ],
        out_specs=pl.BlockSpec((rows, BLK, width), lambda j, *_: (0, j, 0)),
        scratch_shapes=[
            pltpu.VMEM((2, NBR * CELLS, 2 * width), jnp.bfloat16),
            pltpu.SemaphoreType.DMA((2, NBR)),
        ],
    )
    return pl.pallas_call(
        functools.partial(attend_kernel, block_cols),
        grid_spec=grid_spec,
        out_shape=jax.ShapeDtypeStruct((rows, q_grid.shape[1], width), jnp.bfloat16),
        compiler_params=pltpu.CompilerParams(dimension_semantics=("arbitrary",)),
    )(codes.reshape(-1), counts.reshape(-1), live_count.reshape(-1), q_grid, kv_mid, kv_left, kv_right)


def body(tokens, mod_shift, mod_scale, qkv_weight, block_codes, block_counts, valid_tokens):
    tile_rows = tokens.shape[1]
    tile_cols = tokens.shape[2]
    width = HEADS * HD
    group = lax.axis_size("gx")
    me = lax.axis_index("gx")
    tile = tokens[0]
    received = [tile] + [
        lax.ppermute(tile, "gx", [(i, (i + d) % group) for i in range(group)])
        for d in range(1, group)
    ]
    weight_block = lax.all_gather(qkv_weight, "wa", axis=1, tiled=True)
    strip = normalize(jnp.stack(received), mod_shift[0], mod_scale[0]).reshape(
        group, tile_rows * tile_cols, D
    )
    partial = [
        jnp.dot(strip[d], weight_block, preferred_element_type=jnp.float32).astype(jnp.bfloat16)
        for d in range(group)
    ]
    partial[0] = lax.optimization_barrier(partial[0])
    returned = [partial[0]] + [
        lax.ppermute(partial[d], "gx", [(i, (i - d) % group) for i in range(group)])
        for d in range(1, group)
    ]
    rows_axis = lax.axis_size("gy")
    block = partial[0].shape[-1]
    senders = [g for g in range(group) if (g + 1) * block > width]

    def neighbour_rows(step):
        chunks = []
        for d in range(group):
            pairs = [
                (r * group + g, (r + step) * group + (g - d) % group)
                for r in range(rows_axis)
                if 0 <= r + step < rows_axis
                for g in senders
            ]
            chunks.append(lax.ppermute(partial[d], ("gy", "gx"), pairs))
        return assemble(chunks)[:, :, width:]

    def assemble(chunks):
        blocks = []
        for b in range(group):
            pick = (b - me) % group
            chosen = chunks[0]
            for d in range(1, group):
                chosen = jnp.where(pick == d, chunks[d], chosen)
            blocks.append(chosen)
        return jnp.concatenate(blocks, axis=1).reshape(tile_rows, tile_cols, 3 * width)

    above = neighbour_rows(1)
    below = neighbour_rows(-1)
    qkv_grid = assemble(returned)
    middle = to_blocks(jnp.concatenate([above, qkv_grid[:, :, width:], below], axis=0))
    col_up = [(i, i + 1) for i in range(group - 1)]
    col_down = [(i + 1, i) for i in range(group - 1)]
    left = lax.ppermute(middle[:, -1], "gx", col_up)
    right = lax.ppermute(middle[:, 0], "gx", col_down)
    block_rows = tile_rows // BLK
    block_cols = tile_cols // BLK
    queries = to_blocks(qkv_grid[:, :, :width])
    row_ids = jnp.arange(block_rows, dtype=jnp.int32)[:, None, None]
    col_ids = jnp.arange(block_cols, dtype=jnp.int32)[None, :, None]
    row_step = block_codes // 3 - 1
    col_step = block_codes % 3 - 1
    global_row = jnp.clip(
        lax.axis_index("gy") * block_rows + row_ids + row_step, 0, valid_tokens.shape[0] - 1
    )
    global_col = jnp.clip(
        lax.axis_index("gx") * block_cols + col_ids + col_step, 0, valid_tokens.shape[1] - 1
    )
    live_count = valid_tokens[global_row, global_col]
    number = block_rows * block_cols
    result = local_attention(
        qkv_grid,
        middle.reshape(-1, CELLS, 2 * width),
        left,
        right,
        block_codes.reshape(number, NBR),
        block_counts.reshape(number),
        live_count.reshape(number, NBR),
        block_cols,
    )
    return result[None]


def solution(mesh):
    return jax.shard_map(
        body,
        mesh=mesh,
        in_specs=(
            P("wa", "gy", "gx", None),
            P("wa", None),
            P("wa", None),
            P(None, ("gx", "wa")),
            P("gy", "gx", None),
            P("gy", "gx"),
            P(),
        ),
        out_specs=P("wa", "gy", "gx", None),
        check_vma=False,
    )
```
